256 devices in a mesh: seq: 16 (over y, z_hi, core), head: 16 (over x, z_lo).
Axes of the slice: x: 4, y: 4, z: 8 (z_hi: 2, z_lo: 4; z = z_hi * 4 + z_lo), core: 2. Of those that a mesh axis runs over, the one named last changes fastest.
Arguments:
- x_in: bfloat16 [8192, 8192], P('seq', 'head'), may hold values from -6 to 6
- z_in: bfloat16 [8192, 8192], P('seq', 'head'), may hold values from -12 to 12
- bc: bfloat16 [2, 8192, 128], P(None, 'seq'), may hold values from -1.796875 to 1.796875
- dt_raw: float32 [128, 8192], P('head', 'seq'), may hold values from -3 to 3
- dt_bias: float32 [128], P('head'), may hold values from -8 to 0
- decay_rate: float32 [128], P('head'), may hold values from 0.001 to 0.4
- d_skip: float32 [128], P('head'), may hold values from 0.5 to 1.5
- norm_gain: float32 [8192], P('head'), may hold values from 0.1 to 1.9
- out_weight: bfloat16 [8192, 4096], P('head', 'seq'), may hold values from -0.0625 to 0.0625
- resid: bfloat16 [8192, 4096], P(('seq', 'head')), may hold values from -6 to 6
- mlp_gain: float32 [4096], replicated, may hold values from 0.1 to 1.9
- gate_weight: bfloat16 [4096, 8192], P(None, 'head'), may hold values from -0.09375 to 0.09375
- up_weight: bfloat16 [4096, 8192], P(None, 'head'), may hold values from -0.09375 to 0.09375
- down_weight: bfloat16 [8192, 4096], P('head', 'seq'), may hold values from -0.0625 to 0.0625
Outputs:
- layer_out: bfloat16 [8192, 4096], P(('seq', 'head'))
The draws below stay inside these ranges and needn't reach their ends.
All inputs are finite; a program needn't handle non-finite values.
Results may differ from the reference program's by a relative error of at most 0.0075.
Values may be sent and summed in bfloat16 or wider, within the bound.
No kernel may reach another device: no remote copies, remote signals or barrier semaphores. Data moves between devices by JAX's collectives and lax.ppermute only.
A program may use at most 128 MiB of HBM per device.

```python
import math
import jax
import jax.numpy as jnp
from jax import lax

D = 4096
HEADS = 128
HEAD_DIM = 64
STATE = 128
BLOCK = 256
FF = 8192
TOKENS = 8192
INNER = 8192


def head_memory(key):
    split_keys = jax.random.split(jax.random.fold_in(key, 7), 3)
    slow_share = 0.5
    is_slow = jax.random.uniform(split_keys[0], (HEADS,)) < slow_share
    slow_span = TOKENS * jnp.exp(jax.random.uniform(split_keys[1], (HEADS,), minval=math.log(1.5), maxval=math.log(6.0)))
    fast_span = jnp.exp(jax.random.uniform(split_keys[2], (HEADS,), minval=math.log(30.0), maxval=math.log(75.0)))
    return jnp.where(is_slow, slow_span, fast_span)


def draw_decay_rate(key, part):
    memory_span = head_memory(key)
    jitter = jnp.exp(jax.random.uniform(jax.random.fold_in(key, 8), (HEADS,), minval=math.log(0.7), maxval=math.log(1.4)))
    return (jitter / jnp.sqrt(memory_span)).astype(jnp.float32)


def draw_dt_bias(key, part):
    memory_span = head_memory(key)
    jitter = jnp.exp(jax.random.uniform(jax.random.fold_in(key, 9), (HEADS,), minval=math.log(0.7), maxval=math.log(1.4)))
    base_step = jitter / jnp.sqrt(memory_span)
    return jnp.log(jnp.expm1(base_step)).astype(jnp.float32)


def draw_dt_raw(key, part):
    split_keys = jax.random.split(jax.random.fold_in(key, 5), 2)
    offsets = jax.random.uniform(split_keys[0], (TOKENS // BLOCK,), minval=-1.0, maxval=1.0)
    by_position = jnp.repeat(offsets, BLOCK)
    jitter_noise = jnp.clip(0.7 * jax.random.normal(split_keys[1], (HEADS, TOKENS)), -2.0, 2.0)
    return (jitter_noise + by_position[None, :]).astype(jnp.float32)


def draw_z_in(key, part):
    split_keys = jax.random.split(jax.random.fold_in(key, 3), 2)
    position = jnp.arange(HEADS, dtype=jnp.float32) / max(HEADS - 1, 1)
    head_scale = 0.6 * jnp.exp(position * math.log(4.0))
    head_scale = head_scale * jnp.exp(jax.random.uniform(split_keys[0], (HEADS,), minval=math.log(0.8), maxval=math.log(1.25)))
    base_values = jnp.clip(jax.random.normal(split_keys[1], (TOKENS, INNER)), -4.0, 4.0)
    return (base_values * jnp.repeat(head_scale, HEAD_DIM)[None, :]).astype(jnp.bfloat16)


def level_of(rng, extent, shards, smallest, top_value):
    factor_of = 1.0
    for dim, parts in shards:
        steps = jax.random.uniform(jax.random.fold_in(jax.random.fold_in(rng, 6), dim), (parts,), jnp.float32, smallest / len(shards), top_value / len(shards))
        factor_of = factor_of * jnp.repeat(jnp.exp(steps), extent[dim] // parts).reshape((-1,) + (1,) * (len(extent) - 1 - dim))
    return factor_of


def gaussian(stream_key, shape, spread, reach, pieces=(), kind=jnp.bfloat16):
    loudness = level_of(stream_key, shape, pieces, -0.22, 0.18) if pieces else 1.0
    values = jax.random.normal(stream_key, shape, jnp.float32) * spread * loudness
    return jnp.minimum(jnp.maximum(values, -reach), reach).astype(kind)


def setup_inputs(seed: int = 0) -> dict:
    key_of = jax.random.split(jax.random.key(seed), 15)
    return {
        "x_in": gaussian(key_of[0], (TOKENS, INNER), 1.0, 6.0, ((0, 16), (1, 16))),
        "z_in": draw_z_in(jax.random.fold_in(key_of[14], 71), 0),
        "bc": gaussian(key_of[2], (2, TOKENS, STATE), 0.3, 1.796875, ((1, 16),)),
        "dt_raw": draw_dt_raw(jax.random.fold_in(key_of[14], 71), 0),
        "dt_bias": draw_dt_bias(jax.random.fold_in(key_of[14], 71), 0),
        "decay_rate": draw_decay_rate(jax.random.fold_in(key_of[14], 71), 0),
        "d_skip": jnp.clip(0.5 + 1.0 * jax.random.uniform(key_of[6], (HEADS,), jnp.float32) ** level_of(key_of[6], (HEADS,), ((0, 16),), -0.2, 0.2), 0.5, 1.5),
        "norm_gain": jnp.clip(1.0 + 0.18 * jax.random.normal(key_of[7], (INNER,), jnp.float32), 0.1, 1.9),
        "out_weight": gaussian(key_of[8], (INNER, D), INNER ** -0.5, 0.0625, ((0, 16), (1, 16))),
        "resid": gaussian(key_of[9], (TOKENS, D), 1.0, 6.0, ((0, 256),)),
        "mlp_gain": jnp.clip(1.0 + 0.18 * jax.random.normal(key_of[10], (D,), jnp.float32), 0.1, 1.9),
        "gate_weight": gaussian(key_of[11], (D, FF), D ** -0.5, 0.09375, ((1, 16),)),
        "up_weight": gaussian(key_of[12], (D, FF), D ** -0.5, 0.09375, ((1, 16),)),
        "down_weight": gaussian(key_of[13], (FF, D), FF ** -0.5, 0.0625, ((0, 16), (1, 16))),
    }


epsilon = 1e-05

def block_scan(x_heads, b_rows, c_rows, step_size, log_decay, block_len, start_state):
    length, head_count, head_width = x_heads.shape
    state_size = b_rows.shape[1]
    block_count = length // block_len
    x_blocks = x_heads.reshape(block_count, block_len, head_count, head_width)
    b_blocks = b_rows.reshape(block_count, block_len, state_size)
    c_blocks = c_rows.reshape(block_count, block_len, state_size)
    d_blocks = step_size.reshape(head_count, block_count, block_len).transpose(1, 0, 2)
    a_blocks = log_decay.reshape(head_count, block_count, block_len).transpose(1, 0, 2)
    lower_mask = jnp.tril(jnp.ones((block_len, block_len), dtype=bool))

    def advance(carry_state, inputs):
        x_block, b_block, c_block, d_block, a_block = inputs
        cumulative = jnp.cumsum(a_block, axis=1)
        gap_values = jnp.where(lower_mask[None], cumulative[:, :, None] - cumulative[:, None, :], -jnp.inf)
        scores = jnp.dot(c_block, b_block.T, preferred_element_type=jnp.float32)
        mixing = (jnp.exp(gap_values) * scores[None] * d_block[:, None, :]).astype(jnp.bfloat16)
        within = jnp.einsum('hij,jhp->ihp', mixing.astype(jnp.float32), x_block.astype(jnp.float32))
        carried = jnp.einsum('in,hpn->ihp', c_block.astype(jnp.float32), carry_state, precision=lax.Precision.HIGHEST)
        carried = carried * jnp.exp(cumulative).T[:, :, None]
        last_cum = cumulative[:, -1:]
        inject = ((jnp.exp(last_cum - cumulative) * d_block)[:, :, None] * b_block.astype(jnp.float32)[None]).astype(jnp.bfloat16)
        added = jnp.einsum('jhp,hjn->hpn', x_block.astype(jnp.float32), inject.astype(jnp.float32))
        new_state = jnp.exp(last_cum)[:, :, None] * carry_state + added
        return (new_state, within + carried)
    final_state, block_outs = lax.scan(advance, start_state, (x_blocks, b_blocks, c_blocks, d_blocks, a_blocks))
    return (block_outs.reshape(length, head_count, head_width), final_state)

def normalize_rows(layer_sum, mlp_gain):
    mean_square = lax.optimization_barrier(jnp.mean(layer_sum * layer_sum, axis=1, keepdims=True))
    return (layer_sum * lax.rsqrt(mean_square + epsilon) * mlp_gain).astype(jnp.bfloat16)

def reference(x_in, z_in, bc, dt_raw, dt_bias, decay_rate, d_skip, norm_gain, out_weight, resid, mlp_gain, gate_weight, up_weight, down_weight):
    step_size = jax.nn.softplus(dt_raw + dt_bias[:, None])
    log_decay = -decay_rate[:, None] * step_size
    x_heads = x_in.reshape(TOKENS, HEADS, HEAD_DIM)
    zero_state = jnp.zeros((HEADS, HEAD_DIM, STATE), jnp.float32)
    ssd_out, final_state = block_scan(x_heads, bc[0], bc[1], step_size, log_decay, BLOCK, zero_state)
    ssd_out = ssd_out + d_skip[None, :, None] * x_heads.astype(jnp.float32)
    gated_out = ssd_out.reshape(TOKENS, INNER) * jax.nn.silu(z_in.astype(jnp.float32))
    row_squares = lax.optimization_barrier(jnp.sum(gated_out * gated_out, axis=1))
    gated_scaled = (gated_out * norm_gain).astype(jnp.bfloat16)
    projected = jnp.dot(gated_scaled, out_weight, preferred_element_type=jnp.float32)
    layer_sum = resid.astype(jnp.float32) + projected * lax.rsqrt(row_squares / INNER + epsilon)[:, None]
    normed = normalize_rows(layer_sum, mlp_gain)
    gate_part = jnp.dot(normed, gate_weight, preferred_element_type=jnp.float32)
    up_part = jnp.dot(normed, up_weight, preferred_element_type=jnp.float32)
    hidden = (jax.nn.silu(gate_part) * up_part).astype(jnp.bfloat16)
    mlp_out = jnp.dot(hidden, down_weight, preferred_element_type=jnp.float32)
    return (layer_sum + mlp_out).astype(jnp.bfloat16)
```

```python
import jax
import jax.numpy as jnp
from jax import lax
from jax.sharding import PartitionSpec as P

BLOCK = 256
INNER = 8192


epsilon = 1e-05


def passed_along(value, axis, steps):
    count = lax.axis_size(axis)
    initial, last = (max(0, -steps), min(count, count - steps))
    return lax.ppermute(value, axis, [(source, source + steps) for source in range(initial, last)])


def block_scan(x_heads, b_rows, c_rows, step_size, log_decay, block_len):
    length, head_count, head_width = x_heads.shape
    state_size = b_rows.shape[1]
    block_count = length // block_len
    lower_mask = jnp.tril(jnp.ones((block_len, block_len), dtype=bool))
    carry_state = jnp.zeros((head_count, head_width, state_size), jnp.float32)
    outs = []
    for blk in range(block_count):
        rows = slice(blk * block_len, (blk + 1) * block_len)
        x_block = x_heads[rows]
        b_block = b_rows[rows]
        c_block = c_rows[rows]
        d_block = step_size[:, rows]
        a_block = log_decay[:, rows]
        cumulative = jnp.cumsum(a_block, axis=1)
        gap_values = jnp.where(
            lower_mask[None], cumulative[:, :, None] - cumulative[:, None, :], -jnp.inf
        )
        scores = jnp.dot(c_block, b_block.T, preferred_element_type=jnp.float32)
        mixing = (jnp.exp(gap_values) * scores[None] * d_block[:, None, :]).astype(jnp.bfloat16)
        within = jnp.einsum("hij,jhp->ihp", mixing, x_block, preferred_element_type=jnp.float32)
        if blk > 0:
            carried = jnp.einsum(
                "in,hpn->ihp", c_block.astype(jnp.float32), carry_state,
                precision=lax.Precision.HIGHEST,
            )
            within = within + carried * jnp.exp(cumulative).T[:, :, None]
        last_cum = cumulative[:, -1:]
        inject = (
            (jnp.exp(last_cum - cumulative) * d_block)[:, :, None]
            * b_block.astype(jnp.float32)[None]
        ).astype(jnp.bfloat16)
        added = jnp.einsum("jhp,hjn->hpn", x_block, inject, preferred_element_type=jnp.float32)
        carry_state = jnp.exp(last_cum)[:, :, None] * carry_state + added
        outs.append(within)
    return jnp.concatenate(outs, axis=0), carry_state


def entering_state(group_decay, local_state):
    count = lax.axis_size("seq")
    dec = passed_along(group_decay, "seq", 1)
    st = passed_along(local_state, "seq", 1)
    step = 1
    while step < count:
        sp = passed_along(st, "seq", step)
        if step * 2 < count:
            dp = passed_along(dec, "seq", step)
        st = dec[:, None, None] * sp + st
        if step * 2 < count:
            dec = dp * dec
        step *= 2
    return st


def normalize_rows(layer_sum, mlp_gain):
    mean_square = jnp.mean(layer_sum * layer_sum, axis=1, keepdims=True)
    return (layer_sum * lax.rsqrt(mean_square + epsilon) * mlp_gain).astype(jnp.bfloat16)


def shards(
    x_in,
    z_in,
    bc,
    dt_raw,
    dt_bias,
    decay_rate,
    d_skip,
    norm_gain,
    out_weight,
    resid,
    mlp_gain,
    gate_weight,
    up_weight,
    down_weight,
):
    out_full, down_full = (
        lax.all_gather(out_weight, "seq", axis=1, tiled=True),
        lax.all_gather(down_weight, "seq", axis=1, tiled=True),
    )
    head_count = dt_raw.shape[0]
    length = dt_raw.shape[1]
    head_width = x_in.shape[1] // head_count
    step_size = jax.nn.softplus(dt_raw + dt_bias[:, None])
    log_decay = -decay_rate[:, None] * step_size
    x_heads = x_in.reshape(length, head_count, head_width)
    local_out, local_state = block_scan(x_heads, bc[0], bc[1], step_size, log_decay, BLOCK)
    running = jnp.cumsum(log_decay, axis=1)
    group_decay = jnp.exp(running[:, -1])
    entering = entering_state(group_decay, local_state)
    carried = jnp.einsum(
        "tn,hpn->thp", bc[1].astype(jnp.float32), entering, precision=lax.Precision.HIGHEST
    )
    carried = carried * jnp.exp(running).T[:, :, None]
    ssd_out = local_out + carried + d_skip[None, :, None] * x_heads.astype(jnp.float32)
    gated_out = ssd_out.reshape(length, head_count * head_width) * jax.nn.silu(
        z_in.astype(jnp.float32)
    )
    row_squares = jnp.sum(gated_out * gated_out, axis=1)
    gated_scaled = (gated_out * norm_gain).astype(jnp.bfloat16)
    partial_value = jnp.dot(gated_scaled, out_full, preferred_element_type=jnp.float32)
    width = partial_value.shape[1]
    sq_hi = row_squares.astype(jnp.bfloat16)
    sq_lo = (row_squares - sq_hi.astype(jnp.float32)).astype(jnp.bfloat16)
    extra = jnp.zeros((length, 128), jnp.bfloat16).at[:, 0].set(sq_hi).at[:, 1].set(sq_lo)
    packed = jnp.concatenate([partial_value.astype(jnp.bfloat16), extra], axis=1)
    reduced = lax.psum_scatter(packed, "head", scatter_dimension=0, tiled=True)
    part_rows = reduced[:, :width].astype(jnp.float32)
    part_squares = reduced[:, width].astype(jnp.float32) + reduced[:, width + 1].astype(jnp.float32)
    layer_sum = (
        resid.astype(jnp.float32) + part_rows * lax.rsqrt(part_squares / INNER + epsilon)[:, None]
    )
    normed = normalize_rows(layer_sum, mlp_gain)
    rows_piece = lax.all_gather(normed, "head", axis=0, tiled=True)
    gate_part = jnp.dot(rows_piece, gate_weight, preferred_element_type=jnp.float32)
    up_part = jnp.dot(rows_piece, up_weight, preferred_element_type=jnp.float32)
    hidden = (jax.nn.silu(gate_part) * up_part).astype(jnp.bfloat16)
    mlp_part = jnp.dot(hidden, down_full, preferred_element_type=jnp.float32)
    mlp_rows = lax.psum_scatter(
        mlp_part.astype(jnp.bfloat16), "head", scatter_dimension=0, tiled=True
    )
    return (layer_sum + mlp_rows.astype(jnp.float32)).astype(jnp.bfloat16)


def solution(mesh):
    in_specs = (
        P("seq", "head"),
        P("seq", "head"),
        P(None, "seq", None),
        P("head", "seq"),
        P("head"),
        P("head"),
        P("head"),
        P("head"),
        P("head", "seq"),
        P(("seq", "head"), None),
        P(),
        P(None, "head"),
        P(None, "head"),
        P("head", "seq"),
    )
    out_specs = P(("seq", "head"), None)
    return jax.shard_map(shards, mesh=mesh, in_specs=in_specs, out_specs=out_specs, check_vma=False)
```

```python
import jax
import jax.numpy as jnp
from jax import lax
from jax.sharding import PartitionSpec as P

BLOCK = 256
INNER = 8192


epsilon = 1e-05


def passed_along(value, axis, steps):
    count = lax.axis_size(axis)
    initial, last = (max(0, -steps), min(count, count - steps))
    return lax.ppermute(value, axis, [(source, source + steps) for source in range(initial, last)])


def block_scan(x_heads, b_rows, c_rows, step_size, log_decay, block_len):
    length, head_count, head_width = x_heads.shape
    state_size = b_rows.shape[1]
    block_count = length // block_len
    lower_mask = jnp.tril(jnp.ones((block_len, block_len), dtype=bool))
    carry_state = jnp.zeros((head_count, head_width, state_size), jnp.float32)
    outs = []
    for blk in range(block_count):
        rows = slice(blk * block_len, (blk + 1) * block_len)
        x_block = x_heads[rows]
        b_block = b_rows[rows]
        c_block = c_rows[rows]
        d_block = step_size[:, rows]
        a_block = log_decay[:, rows]
        cumulative = jnp.cumsum(a_block, axis=1)
        gap_values = jnp.where(
            lower_mask[None], cumulative[:, :, None] - cumulative[:, None, :], -jnp.inf
        )
        scores = jnp.dot(c_block, b_block.T, preferred_element_type=jnp.float32)
        mixing = (jnp.exp(gap_values) * scores[None] * d_block[:, None, :]).astype(jnp.bfloat16)
        within = jnp.einsum("hij,jhp->ihp", mixing, x_block, preferred_element_type=jnp.float32)
        if blk > 0:
            carried = jnp.einsum(
                "in,hpn->ihp", c_block.astype(jnp.float32), carry_state,
                precision=lax.Precision.HIGHEST,
            )
            within = within + carried * jnp.exp(cumulative).T[:, :, None]
        last_cum = cumulative[:, -1:]
        inject = (
            (jnp.exp(last_cum - cumulative) * d_block)[:, :, None]
            * b_block.astype(jnp.float32)[None]
        ).astype(jnp.bfloat16)
        added = jnp.einsum("jhp,hjn->hpn", x_block, inject, preferred_element_type=jnp.float32)
        carry_state = jnp.exp(last_cum)[:, :, None] * carry_state + added
        outs.append(within)
    return jnp.concatenate(outs, axis=0), carry_state


def entering_state(group_decay, local_state):
    count = lax.axis_size("seq")
    dec = passed_along(group_decay, "seq", 1)
    st = passed_along(local_state, "seq", 1)
    step = 1
    while step < count:
        sp = passed_along(st, "seq", step)
        if step * 2 < count:
            dp = passed_along(dec, "seq", step)
        st = dec[:, None, None] * sp + st
        if step * 2 < count:
            dec = dp * dec
        step *= 2
    return st


def sum_over_head(value):
    count = lax.axis_size("head")
    pieces = value.reshape(count, value.shape[0] // count, value.shape[1])
    pieces = lax.all_to_all(pieces, "head", 0, 0, tiled=False)
    return jnp.sum(pieces.astype(jnp.float32), axis=0)


def normalize_rows(layer_sum, mlp_gain):
    mean_square = jnp.mean(layer_sum * layer_sum, axis=1, keepdims=True)
    return (layer_sum * lax.rsqrt(mean_square + epsilon) * mlp_gain).astype(jnp.bfloat16)


def shards(
    x_in,
    z_in,
    bc,
    dt_raw,
    dt_bias,
    decay_rate,
    d_skip,
    norm_gain,
    out_weight,
    resid,
    mlp_gain,
    gate_weight,
    up_weight,
    down_weight,
):
    out_full, down_full = (
        lax.all_gather(out_weight, "seq", axis=1, tiled=True),
        lax.all_gather(down_weight, "seq", axis=1, tiled=True),
    )
    head_count = dt_raw.shape[0]
    length = dt_raw.shape[1]
    head_width = x_in.shape[1] // head_count
    step_size = jax.nn.softplus(dt_raw + dt_bias[:, None])
    log_decay = -decay_rate[:, None] * step_size
    x_heads = x_in.reshape(length, head_count, head_width)
    local_out, local_state = block_scan(x_heads, bc[0], bc[1], step_size, log_decay, BLOCK)
    running = jnp.cumsum(log_decay, axis=1)
    group_decay = jnp.exp(running[:, -1])
    entering = entering_state(group_decay, local_state)
    carried = jnp.einsum(
        "tn,hpn->thp", bc[1].astype(jnp.float32), entering, precision=lax.Precision.HIGHEST
    )
    carried = carried * jnp.exp(running).T[:, :, None]
    ssd_out = local_out + carried + d_skip[None, :, None] * x_heads.astype(jnp.float32)
    gated_out = ssd_out.reshape(length, head_count * head_width) * jax.nn.silu(
        z_in.astype(jnp.float32)
    )
    row_squares = jnp.sum(gated_out * gated_out, axis=1)
    gated_scaled = (gated_out * norm_gain).astype(jnp.bfloat16)
    partial_value = jnp.dot(gated_scaled, out_full, preferred_element_type=jnp.float32)
    width = partial_value.shape[1]
    sq_hi = row_squares.astype(jnp.bfloat16)
    sq_lo = (row_squares - sq_hi.astype(jnp.float32)).astype(jnp.bfloat16)
    extra = jnp.zeros((length, 128), jnp.bfloat16).at[:, 0].set(sq_hi).at[:, 1].set(sq_lo)
    packed = jnp.concatenate([partial_value.astype(jnp.bfloat16), extra], axis=1)
    reduced = sum_over_head(packed)
    reduced, down_full = lax.optimization_barrier((reduced, down_full))
    part_rows = reduced[:, :width]
    part_squares = reduced[:, width] + reduced[:, width + 1]
    layer_sum = (
        resid.astype(jnp.float32) + part_rows * lax.rsqrt(part_squares / INNER + epsilon)[:, None]
    )
    normed = normalize_rows(layer_sum, mlp_gain)
    rows_piece = lax.all_gather(normed, "head", axis=0, tiled=True)
    gate_part = jnp.dot(rows_piece, gate_weight, preferred_element_type=jnp.float32)
    up_part = jnp.dot(rows_piece, up_weight, preferred_element_type=jnp.float32)
    hidden = (jax.nn.silu(gate_part) * up_part).astype(jnp.bfloat16)
    mlp_part = jnp.dot(hidden, down_full, preferred_element_type=jnp.float32)
    mlp_rows = sum_over_head(mlp_part.astype(jnp.bfloat16))
    return (layer_sum + mlp_rows).astype(jnp.bfloat16)


def solution(mesh):
    in_specs = (
        P("seq", "head"),
        P("seq", "head"),
        P(None, "seq", None),
        P("head", "seq"),
        P("head"),
        P("head"),
        P("head"),
        P("head"),
        P("head", "seq"),
        P(("seq", "head"), None),
        P(),
        P(None, "head"),
        P(None, "head"),
        P("head", "seq"),
    )
    out_specs = P(("seq", "head"), None)
    return jax.shard_map(shards, mesh=mesh, in_specs=in_specs, out_specs=out_specs, check_vma=False)
```

```python
import jax
import jax.numpy as jnp
from jax import lax
from jax.sharding import PartitionSpec as P

BLOCK = 256
INNER = 8192


epsilon = 1e-05


def passed_along(value, axis, steps):
    count = lax.axis_size(axis)
    initial, last = (max(0, -steps), min(count, count - steps))
    return lax.ppermute(value, axis, [(source, source + steps) for source in range(initial, last)])


def block_scan(x_heads, b_rows, c_rows, step_size, log_decay, block_len):
    length, head_count, head_width = x_heads.shape
    state_size = b_rows.shape[1]
    block_count = length // block_len
    lower_mask = jnp.tril(jnp.ones((block_len, block_len), dtype=bool))
    carry_state = jnp.zeros((head_count, head_width, state_size), jnp.float32)
    outs = []
    for blk in range(block_count):
        rows = slice(blk * block_len, (blk + 1) * block_len)
        x_block = x_heads[rows]
        b_block = b_rows[rows]
        c_block = c_rows[rows]
        d_block = step_size[:, rows]
        a_block = log_decay[:, rows]
        cumulative = jnp.cumsum(a_block, axis=1)
        gap_values = jnp.where(
            lower_mask[None], cumulative[:, :, None] - cumulative[:, None, :], -jnp.inf
        )
        scores = jnp.dot(c_block, b_block.T, preferred_element_type=jnp.float32)
        mixing = (jnp.exp(gap_values) * scores[None] * d_block[:, None, :]).astype(jnp.bfloat16)
        within = jnp.einsum("hij,jhp->ihp", mixing, x_block, preferred_element_type=jnp.float32)
        if blk > 0:
            carried = jnp.einsum(
                "in,hpn->ihp", c_block.astype(jnp.float32), carry_state,
                precision=lax.Precision.HIGHEST,
            )
            within = within + carried * jnp.exp(cumulative).T[:, :, None]
        last_cum = cumulative[:, -1:]
        inject = (
            (jnp.exp(last_cum - cumulative) * d_block)[:, :, None]
            * b_block.astype(jnp.float32)[None]
        ).astype(jnp.bfloat16)
        added = jnp.einsum("jhp,hjn->hpn", x_block, inject, preferred_element_type=jnp.float32)
        carry_state = jnp.exp(last_cum)[:, :, None] * carry_state + added
        outs.append(within)
    return jnp.concatenate(outs, axis=0), carry_state


def entering_state(group_decay, local_state):
    count = lax.axis_size("seq")
    dec = passed_along(group_decay, "seq", 1)
    st = passed_along(local_state, "seq", 1)
    step = 1
    while step < count:
        sp = passed_along(st, "seq", step)
        if step * 2 < count:
            dp = passed_along(dec, "seq", step)
        st = dec[:, None, None] * sp + st
        if step * 2 < count:
            dec = dp * dec
        step *= 2
    return st


def sum_over_head(value):
    count = lax.axis_size("head")
    pieces = value.reshape(count, value.shape[0] // count, value.shape[1])
    pieces = lax.all_to_all(pieces, "head", 0, 0, tiled=False)
    return jnp.sum(pieces.astype(jnp.float32), axis=0)


def normalize_rows(layer_sum, mlp_gain):
    mean_square = jnp.mean(layer_sum * layer_sum, axis=1, keepdims=True)
    return (layer_sum * lax.rsqrt(mean_square + epsilon) * mlp_gain).astype(jnp.bfloat16)


def shards(
    x_in,
    z_in,
    bc,
    dt_raw,
    dt_bias,
    decay_rate,
    d_skip,
    norm_gain,
    out_weight,
    resid,
    mlp_gain,
    gate_weight,
    up_weight,
    down_weight,
):
    out_full, down_full = (
        lax.all_gather(out_weight, "seq", axis=1, tiled=True),
        lax.all_gather(down_weight, "seq", axis=1, tiled=True),
    )
    head_count = dt_raw.shape[0]
    length = dt_raw.shape[1]
    head_width = x_in.shape[1] // head_count
    step_size = jax.nn.softplus(dt_raw + dt_bias[:, None])
    log_decay = -decay_rate[:, None] * step_size
    x_heads = x_in.reshape(length, head_count, head_width)
    local_out, local_state = block_scan(x_heads, bc[0], bc[1], step_size, log_decay, BLOCK)
    running = jnp.cumsum(log_decay, axis=1)
    group_decay = jnp.exp(running[:, -1])
    entering = entering_state(group_decay, local_state)
    carried = jnp.einsum(
        "tn,hpn->thp", bc[1].astype(jnp.float32), entering, precision=lax.Precision.HIGHEST
    )
    carried = carried * jnp.exp(running).T[:, :, None]
    ssd_out = local_out + carried + d_skip[None, :, None] * x_heads.astype(jnp.float32)
    gated_out = ssd_out.reshape(length, head_count * head_width) * jax.nn.silu(
        z_in.astype(jnp.float32)
    )
    row_squares = jnp.sum(gated_out * gated_out, axis=1)
    gated_scaled = (gated_out * norm_gain).astype(jnp.bfloat16)
    head_n = lax.axis_size("head")
    chunks = 2
    rows_per = length // head_n // chunks
    width = out_full.shape[1]
    gated_parts = gated_scaled.reshape(head_n, chunks, rows_per, -1)
    square_parts = row_squares.reshape(head_n, chunks, rows_per)
    resid_parts = resid.reshape(chunks, rows_per, -1)

    def packed_rows(chunk):
        chunk_rows = gated_parts[:, chunk].reshape(head_n * rows_per, -1)
        chunk_squares = square_parts[:, chunk].reshape(head_n * rows_per)
        partial_value = jnp.dot(chunk_rows, out_full, preferred_element_type=jnp.float32)
        sq_hi = chunk_squares.astype(jnp.bfloat16)
        sq_lo = (chunk_squares - sq_hi.astype(jnp.float32)).astype(jnp.bfloat16)
        extra = (
            jnp.zeros((head_n * rows_per, 128), jnp.bfloat16).at[:, 0].set(sq_hi).at[:, 1].set(sq_lo)
        )
        return jnp.concatenate([partial_value.astype(jnp.bfloat16), extra], axis=1)

    def finish_rows(reduced, chunk):
        part_rows = reduced[:, :width]
        part_squares = reduced[:, width] + reduced[:, width + 1]
        layer_sum = (
            resid_parts[chunk].astype(jnp.float32)
            + part_rows * lax.rsqrt(part_squares / INNER + epsilon)[:, None]
        )
        return layer_sum, normalize_rows(layer_sum, mlp_gain)

    def mlp_rows(rows_piece, down_full):
        gate_part = jnp.dot(rows_piece, gate_weight, preferred_element_type=jnp.float32)
        up_part = jnp.dot(rows_piece, up_weight, preferred_element_type=jnp.float32)
        hidden = (jax.nn.silu(gate_part) * up_part).astype(jnp.bfloat16)
        mlp_part = jnp.dot(hidden, down_full, preferred_element_type=jnp.float32)
        return sum_over_head(mlp_part.astype(jnp.bfloat16))

    packs = [packed_rows(chunk) for chunk in range(chunks)]
    normed_rows = []
    sums = []
    for chunk in range(chunks):
        pack = packs[chunk]
        if chunk > 0:
            pack, normed_rows[-1] = lax.optimization_barrier((pack, normed_rows[-1]))
        reduced = sum_over_head(pack)
        if chunk == 0:
            reduced, down_full = lax.optimization_barrier((reduced, down_full))
        layer_sum, normed = finish_rows(reduced, chunk)
        sums.append(layer_sum)
        normed_rows.append(normed)
    gathered = []
    for chunk in range(chunks):
        gathered.append(lax.all_gather(normed_rows[chunk], "head", axis=0, tiled=True))
        if chunk + 1 < chunks:
            gathered[-1], normed_rows[chunk + 1] = lax.optimization_barrier(
                (gathered[-1], normed_rows[chunk + 1])
            )
    outs = [sums[c] + mlp_rows(gathered[c], down_full) for c in range(chunks)]
    return jnp.concatenate(outs, axis=0).astype(jnp.bfloat16)


def solution(mesh):
    in_specs = (
        P("seq", "head"),
        P("seq", "head"),
        P(None, "seq", None),
        P("head", "seq"),
        P("head"),
        P("head"),
        P("head"),
        P("head"),
        P("head", "seq"),
        P(("seq", "head"), None),
        P(),
        P(None, "head"),
        P(None, "head"),
        P("head", "seq"),
    )
    out_specs = P(("seq", "head"), None)
    return jax.shard_map(shards, mesh=mesh, in_specs=in_specs, out_specs=out_specs, check_vma=False)
```

```python
import jax
import jax.numpy as jnp
from jax import lax
from jax.sharding import PartitionSpec as P

BLOCK = 256
INNER = 8192


epsilon = 1e-05


def passed_along(value, axis, steps):
    count = lax.axis_size(axis)
    initial, last = (max(0, -steps), min(count, count - steps))
    return lax.ppermute(value, axis, [(source, source + steps) for source in range(initial, last)])


def block_scan(x_heads, b_rows, c_rows, step_size, log_decay, block_len):
    length, head_count, head_width = x_heads.shape
    state_size = b_rows.shape[1]
    block_count = length // block_len
    lower_mask = jnp.tril(jnp.ones((block_len, block_len), dtype=bool))
    carry_state = jnp.zeros((head_count, head_width, state_size), jnp.float32)
    outs = []
    for blk in range(block_count):
        rows = slice(blk * block_len, (blk + 1) * block_len)
        x_block = x_heads[rows]
        b_block = b_rows[rows]
        c_block = c_rows[rows]
        d_block = step_size[:, rows]
        a_block = log_decay[:, rows]
        cumulative = jnp.cumsum(a_block, axis=1)
        gap_values = jnp.where(
            lower_mask[None], cumulative[:, :, None] - cumulative[:, None, :], -jnp.inf
        )
        scores = jnp.dot(c_block, b_block.T, preferred_element_type=jnp.float32)
        mixing = (jnp.exp(gap_values) * scores[None] * d_block[:, None, :]).astype(jnp.bfloat16)
        within = jnp.einsum("hij,jhp->ihp", mixing, x_block, preferred_element_type=jnp.float32)
        if blk > 0:
            carried = jnp.einsum(
                "in,hpn->ihp", c_block.astype(jnp.float32), carry_state,
                precision=lax.Precision.HIGHEST,
            )
            within = within + carried * jnp.exp(cumulative).T[:, :, None]
        last_cum = cumulative[:, -1:]
        inject = (
            (jnp.exp(last_cum - cumulative) * d_block)[:, :, None]
            * b_block.astype(jnp.float32)[None]
        ).astype(jnp.bfloat16)
        added = jnp.einsum("jhp,hjn->hpn", x_block, inject, preferred_element_type=jnp.float32)
        carry_state = jnp.exp(last_cum)[:, :, None] * carry_state + added
        outs.append(within)
    return jnp.concatenate(outs, axis=0), carry_state


def entering_state(group_decay, local_state):
    count = lax.axis_size("seq")
    dec = passed_along(group_decay, "seq", 1)
    st = passed_along(local_state, "seq", 1)
    step = 1
    while step < count:
        sp = passed_along(st, "seq", step)
        if step * 2 < count:
            dp = passed_along(dec, "seq", step)
        st = dec[:, None, None] * sp + st
        if step * 2 < count:
            dec = dp * dec
        step *= 2
    return st


def sum_over_head(value):
    nx, nz = lax.axis_size("hx"), lax.axis_size("hz")
    pieces = value.reshape(nx, nz, value.shape[0] // (nx * nz), value.shape[1])
    pieces = lax.all_to_all(pieces, "hx", 0, 0, tiled=False)
    pieces = jnp.sum(pieces.astype(jnp.float32), axis=0).astype(jnp.bfloat16)
    pieces = lax.all_to_all(pieces, "hz", 0, 0, tiled=False)
    return jnp.sum(pieces.astype(jnp.float32), axis=0)


def gather_over_head(value):
    value = lax.all_gather(value, "hz", axis=0, tiled=True)
    return lax.all_gather(value, "hx", axis=0, tiled=True)


def normalize_rows(layer_sum, mlp_gain):
    mean_square = jnp.mean(layer_sum * layer_sum, axis=1, keepdims=True)
    return (layer_sum * lax.rsqrt(mean_square + epsilon) * mlp_gain).astype(jnp.bfloat16)


def shards(
    x_in,
    z_in,
    bc,
    dt_raw,
    dt_bias,
    decay_rate,
    d_skip,
    norm_gain,
    out_weight,
    resid,
    mlp_gain,
    gate_weight,
    up_weight,
    down_weight,
):
    out_full, down_full = (
        lax.all_gather(out_weight, "seq", axis=1, tiled=True),
        lax.all_gather(down_weight, "seq", axis=1, tiled=True),
    )
    head_count = dt_raw.shape[0]
    length = dt_raw.shape[1]
    head_width = x_in.shape[1] // head_count
    step_size = jax.nn.softplus(dt_raw + dt_bias[:, None])
    log_decay = -decay_rate[:, None] * step_size
    x_heads = x_in.reshape(length, head_count, head_width)
    local_out, local_state = block_scan(x_heads, bc[0], bc[1], step_size, log_decay, BLOCK)
    running = jnp.cumsum(log_decay, axis=1)
    group_decay = jnp.exp(running[:, -1])
    entering = entering_state(group_decay, local_state)
    carried = jnp.einsum(
        "tn,hpn->thp", bc[1].astype(jnp.float32), entering, precision=lax.Precision.HIGHEST
    )
    carried = carried * jnp.exp(running).T[:, :, None]
    ssd_out = local_out + carried + d_skip[None, :, None] * x_heads.astype(jnp.float32)
    gated_out = ssd_out.reshape(length, head_count * head_width) * jax.nn.silu(
        z_in.astype(jnp.float32)
    )
    row_squares = jnp.sum(gated_out * gated_out, axis=1)
    gated_scaled = (gated_out * norm_gain).astype(jnp.bfloat16)
    head_n = lax.axis_size("hx") * lax.axis_size("hz")
    chunks = 2
    rows_per = length // head_n // chunks
    width = out_full.shape[1]
    gated_parts = gated_scaled.reshape(head_n, chunks, rows_per, -1)
    square_parts = row_squares.reshape(head_n, chunks, rows_per)
    resid_parts = resid.reshape(chunks, rows_per, -1)

    def packed_rows(chunk):
        chunk_rows = gated_parts[:, chunk].reshape(head_n * rows_per, -1)
        chunk_squares = square_parts[:, chunk].reshape(head_n * rows_per)
        partial_value = jnp.dot(chunk_rows, out_full, preferred_element_type=jnp.float32)
        sq_hi = chunk_squares.astype(jnp.bfloat16)
        sq_lo = (chunk_squares - sq_hi.astype(jnp.float32)).astype(jnp.bfloat16)
        extra = (
            jnp.zeros((head_n * rows_per, 128), jnp.bfloat16).at[:, 0].set(sq_hi).at[:, 1].set(sq_lo)
        )
        return jnp.concatenate([partial_value.astype(jnp.bfloat16), extra], axis=1)

    def finish_rows(reduced, chunk):
        part_rows = reduced[:, :width]
        part_squares = reduced[:, width] + reduced[:, width + 1]
        layer_sum = (
            resid_parts[chunk].astype(jnp.float32)
            + part_rows * lax.rsqrt(part_squares / INNER + epsilon)[:, None]
        )
        return layer_sum, normalize_rows(layer_sum, mlp_gain)

    def mlp_rows(rows_piece, down_full):
        gate_part = jnp.dot(rows_piece, gate_weight, preferred_element_type=jnp.float32)
        up_part = jnp.dot(rows_piece, up_weight, preferred_element_type=jnp.float32)
        hidden = (jax.nn.silu(gate_part) * up_part).astype(jnp.bfloat16)
        mlp_part = jnp.dot(hidden, down_full, preferred_element_type=jnp.float32)
        return sum_over_head(mlp_part.astype(jnp.bfloat16))

    packs = [packed_rows(chunk) for chunk in range(chunks)]
    normed_rows = []
    sums = []
    for chunk in range(chunks):
        pack = packs[chunk]
        if chunk > 0:
            pack, normed_rows[-1] = lax.optimization_barrier((pack, normed_rows[-1]))
        reduced = sum_over_head(pack)
        if chunk == 0:
            reduced, down_full = lax.optimization_barrier((reduced, down_full))
        layer_sum, normed = finish_rows(reduced, chunk)
        sums.append(layer_sum)
        normed_rows.append(normed)
    gathered = []
    for chunk in range(chunks):
        gathered.append(gather_over_head(normed_rows[chunk]))
        if chunk + 1 < chunks:
            gathered[-1], normed_rows[chunk + 1] = lax.optimization_barrier(
                (gathered[-1], normed_rows[chunk + 1])
            )
    outs = [sums[c] + mlp_rows(gathered[c], down_full) for c in range(chunks)]
    return jnp.concatenate(outs, axis=0).astype(jnp.bfloat16)


def solution(mesh):
    devices = mesh.devices.reshape(mesh.devices.shape[0], 4, mesh.devices.shape[1] // 4)
    mesh = jax.sharding.Mesh(devices, ("seq", "hx", "hz"))
    head = ("hx", "hz")
    in_specs = (
        P("seq", head),
        P("seq", head),
        P(None, "seq", None),
        P(head, "seq"),
        P(head),
        P(head),
        P(head),
        P(head),
        P(head, "seq"),
        P(("seq", "hx", "hz"), None),
        P(),
        P(None, head),
        P(None, head),
        P(head, "seq"),
    )
    out_specs = P(("seq", "hx", "hz"), None)
    return jax.shard_map(shards, mesh=mesh, in_specs=in_specs, out_specs=out_specs, check_vma=False)
```

```python
import jax
import jax.numpy as jnp
from jax import lax
from jax.sharding import PartitionSpec as P

BLOCK = 256
INNER = 8192


epsilon = 1e-05


SEQ = ("sy", "sz", "sc")


def passed_along(value, axis, steps):
    count = 1
    for name in axis:
        count *= lax.axis_size(name)
    initial, last = (max(0, -steps), min(count, count - steps))
    return lax.ppermute(value, axis, [(source, source + steps) for source in range(initial, last)])


def block_scan(x_heads, b_rows, c_rows, step_size, log_decay, block_len):
    length, head_count, head_width = x_heads.shape
    state_size = b_rows.shape[1]
    block_count = length // block_len
    lower_mask = jnp.tril(jnp.ones((block_len, block_len), dtype=bool))
    carry_state = jnp.zeros((head_count, head_width, state_size), jnp.float32)
    outs = []
    for blk in range(block_count):
        rows = slice(blk * block_len, (blk + 1) * block_len)
        x_block = x_heads[rows]
        b_block = b_rows[rows]
        c_block = c_rows[rows]
        d_block = step_size[:, rows]
        a_block = log_decay[:, rows]
        cumulative = jnp.cumsum(a_block, axis=1)
        gap_values = jnp.where(
            lower_mask[None], cumulative[:, :, None] - cumulative[:, None, :], -jnp.inf
        )
        scores = jnp.dot(c_block, b_block.T, preferred_element_type=jnp.float32)
        mixing = (jnp.exp(gap_values) * scores[None] * d_block[:, None, :]).astype(jnp.bfloat16)
        within = jnp.einsum("hij,jhp->ihp", mixing, x_block, preferred_element_type=jnp.float32)
        if blk > 0:
            carried = jnp.einsum(
                "in,hpn->ihp", c_block.astype(jnp.float32), carry_state,
                precision=lax.Precision.HIGHEST,
            )
            within = within + carried * jnp.exp(cumulative).T[:, :, None]
        last_cum = cumulative[:, -1:]
        inject = (
            (jnp.exp(last_cum - cumulative) * d_block)[:, :, None]
            * b_block.astype(jnp.float32)[None]
        ).astype(jnp.bfloat16)
        added = jnp.einsum("jhp,hjn->hpn", x_block, inject, preferred_element_type=jnp.float32)
        carry_state = jnp.exp(last_cum)[:, :, None] * carry_state + added
        outs.append(within)
    return jnp.concatenate(outs, axis=0), carry_state


def entering_state(group_decay, local_state):
    count = 1
    for name in SEQ:
        count *= lax.axis_size(name)
    dec = passed_along(group_decay, SEQ, 1)
    st = passed_along(local_state, SEQ, 1)
    step = 1
    while step < count:
        sp = passed_along(st, SEQ, step)
        if step * 2 < count:
            dp = passed_along(dec, SEQ, step)
        st = dec[:, None, None] * sp + st
        if step * 2 < count:
            dec = dp * dec
        step *= 2
    return st


def sum_over_head(value):
    nx, nz = lax.axis_size("hx"), lax.axis_size("hz")
    pieces = value.reshape(nx, nz, value.shape[0] // (nx * nz), value.shape[1])
    pieces = lax.all_to_all(pieces, "hx", 0, 0, tiled=False)
    pieces = jnp.sum(pieces.astype(jnp.float32), axis=0).astype(jnp.bfloat16)
    pieces = lax.all_to_all(pieces, "hz", 0, 0, tiled=False)
    return jnp.sum(pieces.astype(jnp.float32), axis=0)


def gather_seq_columns(value):
    rows, cols = value.shape
    value = lax.all_gather(value, ("sy", "sz"), axis=0, tiled=False)
    value = lax.all_gather(value, "sc", axis=0, tiled=False)
    value = value.transpose(2, 1, 0, 3)
    return value.reshape(rows, -1)


def gather_over_head(value):
    value = lax.all_gather(value, "hz", axis=0, tiled=True)
    return lax.all_gather(value, "hx", axis=0, tiled=True)


def normalize_rows(layer_sum, mlp_gain):
    mean_square = jnp.mean(layer_sum * layer_sum, axis=1, keepdims=True)
    return (layer_sum * lax.rsqrt(mean_square + epsilon) * mlp_gain).astype(jnp.bfloat16)


def shards(
    x_in,
    z_in,
    bc,
    dt_raw,
    dt_bias,
    decay_rate,
    d_skip,
    norm_gain,
    out_weight,
    resid,
    mlp_gain,
    gate_weight,
    up_weight,
    down_weight,
):
    out_full, down_full = (
        gather_seq_columns(out_weight),
        gather_seq_columns(down_weight),
    )
    head_count = dt_raw.shape[0]
    length = dt_raw.shape[1]
    head_width = x_in.shape[1] // head_count
    step_size = jax.nn.softplus(dt_raw + dt_bias[:, None])
    log_decay = -decay_rate[:, None] * step_size
    x_heads = x_in.reshape(length, head_count, head_width)
    local_out, local_state = block_scan(x_heads, bc[0], bc[1], step_size, log_decay, BLOCK)
    running = jnp.cumsum(log_decay, axis=1)
    group_decay = jnp.exp(running[:, -1])
    entering = entering_state(group_decay, local_state)
    carried = jnp.einsum(
        "tn,hpn->thp", bc[1].astype(jnp.float32), entering, precision=lax.Precision.HIGHEST
    )
    carried = carried * jnp.exp(running).T[:, :, None]
    ssd_out = local_out + carried + d_skip[None, :, None] * x_heads.astype(jnp.float32)
    gated_out = ssd_out.reshape(length, head_count * head_width) * jax.nn.silu(
        z_in.astype(jnp.float32)
    )
    row_squares = jnp.sum(gated_out * gated_out, axis=1)
    gated_scaled = (gated_out * norm_gain).astype(jnp.bfloat16)
    head_n = lax.axis_size("hx") * lax.axis_size("hz")
    chunks = 2
    rows_per = length // head_n // chunks
    width = out_full.shape[1]
    gated_parts = gated_scaled.reshape(head_n, chunks, rows_per, -1)
    square_parts = row_squares.reshape(head_n, chunks, rows_per)
    resid_parts = resid.reshape(chunks, rows_per, -1)

    def packed_rows(chunk):
        chunk_rows = gated_parts[:, chunk].reshape(head_n * rows_per, -1)
        chunk_squares = square_parts[:, chunk].reshape(head_n * rows_per)
        partial_value = jnp.dot(chunk_rows, out_full, preferred_element_type=jnp.float32)
        sq_hi = chunk_squares.astype(jnp.bfloat16)
        sq_lo = (chunk_squares - sq_hi.astype(jnp.float32)).astype(jnp.bfloat16)
        extra = (
            jnp.zeros((head_n * rows_per, 128), jnp.bfloat16).at[:, 0].set(sq_hi).at[:, 1].set(sq_lo)
        )
        return jnp.concatenate([partial_value.astype(jnp.bfloat16), extra], axis=1)

    def finish_rows(reduced, chunk):
        part_rows = reduced[:, :width]
        part_squares = reduced[:, width] + reduced[:, width + 1]
        layer_sum = (
            resid_parts[chunk].astype(jnp.float32)
            + part_rows * lax.rsqrt(part_squares / INNER + epsilon)[:, None]
        )
        return layer_sum, normalize_rows(layer_sum, mlp_gain)

    def mlp_rows(rows_piece, down_full):
        gate_part = jnp.dot(rows_piece, gate_weight, preferred_element_type=jnp.float32)
        up_part = jnp.dot(rows_piece, up_weight, preferred_element_type=jnp.float32)
        hidden = (jax.nn.silu(gate_part) * up_part).astype(jnp.bfloat16)
        mlp_part = jnp.dot(hidden, down_full, preferred_element_type=jnp.float32)
        return sum_over_head(mlp_part.astype(jnp.bfloat16))

    packs = [packed_rows(chunk) for chunk in range(chunks)]
    normed_rows = []
    sums = []
    for chunk in range(chunks):
        pack = packs[chunk]
        if chunk > 0:
            pack, normed_rows[-1] = lax.optimization_barrier((pack, normed_rows[-1]))
        reduced = sum_over_head(pack)
        if chunk == 0:
            reduced, down_full = lax.optimization_barrier((reduced, down_full))
        layer_sum, normed = finish_rows(reduced, chunk)
        sums.append(layer_sum)
        normed_rows.append(normed)
    gathered = []
    for chunk in range(chunks):
        gathered.append(gather_over_head(normed_rows[chunk]))
        if chunk + 1 < chunks:
            gathered[-1], normed_rows[chunk + 1] = lax.optimization_barrier(
                (gathered[-1], normed_rows[chunk + 1])
            )
    outs = [sums[c] + mlp_rows(gathered[c], down_full) for c in range(chunks)]
    return jnp.concatenate(outs, axis=0).astype(jnp.bfloat16)


def solution(mesh):
    seq_n, head_n = mesh.devices.shape
    devices = mesh.devices.reshape(seq_n // 4, 2, 2, 4, head_n // 4)
    mesh = jax.sharding.Mesh(devices, ("sy", "sz", "sc", "hx", "hz"))
    head = ("hx", "hz")
    in_specs = (
        P(SEQ, head),
        P(SEQ, head),
        P(None, SEQ, None),
        P(head, SEQ),
        P(head),
        P(head),
        P(head),
        P(head),
        P(head, SEQ),
        P(SEQ + head, None),
        P(),
        P(None, head),
        P(None, head),
        P(head, SEQ),
    )
    out_specs = P(SEQ + head, None)
    return jax.shard_map(shards, mesh=mesh, in_specs=in_specs, out_specs=out_specs, check_vma=False)
```

```python
import jax
import jax.numpy as jnp
from jax import lax
from jax.sharding import PartitionSpec as P

BLOCK = 256
INNER = 8192


epsilon = 1e-05


def passed_along(value, axis, steps):
    count = lax.axis_size(axis)
    initial, last = (max(0, -steps), min(count, count - steps))
    return lax.ppermute(value, axis, [(source, source + steps) for source in range(initial, last)])


def block_scan(x_heads, b_rows, c_rows, step_size, log_decay, block_len):
    length, head_count, head_width = x_heads.shape
    state_size = b_rows.shape[1]
    block_count = length // block_len
    lower_mask = jnp.tril(jnp.ones((block_len, block_len), dtype=bool))
    carry_state = jnp.zeros((head_count, head_width, state_size), jnp.float32)
    outs = []
    for blk in range(block_count):
        rows = slice(blk * block_len, (blk + 1) * block_len)
        x_block = x_heads[rows]
        b_block = b_rows[rows]
        c_block = c_rows[rows]
        d_block = step_size[:, rows]
        a_block = log_decay[:, rows]
        cumulative = jnp.cumsum(a_block, axis=1)
        gap_values = jnp.where(
            lower_mask[None], cumulative[:, :, None] - cumulative[:, None, :], -jnp.inf
        )
        scores = jnp.dot(c_block, b_block.T, preferred_element_type=jnp.float32)
        mixing = (jnp.exp(gap_values) * scores[None] * d_block[:, None, :]).astype(jnp.bfloat16)
        within = jnp.einsum("hij,jhp->ihp", mixing, x_block, preferred_element_type=jnp.float32)
        if blk > 0:
            carried = jnp.einsum(
                "in,hpn->ihp", c_block.astype(jnp.float32), carry_state,
                precision=lax.Precision.HIGHEST,
            )
            within = within + carried * jnp.exp(cumulative).T[:, :, None]
        last_cum = cumulative[:, -1:]
        inject = (
            (jnp.exp(last_cum - cumulative) * d_block)[:, :, None]
            * b_block.astype(jnp.float32)[None]
        ).astype(jnp.bfloat16)
        added = jnp.einsum("jhp,hjn->hpn", x_block, inject, preferred_element_type=jnp.float32)
        carry_state = jnp.exp(last_cum)[:, :, None] * carry_state + added
        outs.append(within)
    return jnp.concatenate(outs, axis=0), carry_state


def entering_state(group_decay, local_state):
    count = lax.axis_size("seq")
    dec = passed_along(group_decay, "seq", 1)
    st = passed_along(local_state, "seq", 1)
    step = 1
    while step < count:
        sp = passed_along(st, "seq", step)
        if step * 2 < count:
            dp = passed_along(dec, "seq", step)
        st = dec[:, None, None] * sp + st
        if step * 2 < count:
            dec = dp * dec
        step *= 2
    return st


def sum_over_head(value):
    nx, nz = lax.axis_size("hx"), lax.axis_size("hz")
    pieces = value.reshape(nx, nz, value.shape[0] // (nx * nz), value.shape[1])
    pieces = lax.all_to_all(pieces, "hx", 0, 0, tiled=False)
    pieces = jnp.sum(pieces.astype(jnp.float32), axis=0).astype(jnp.bfloat16)
    pieces = lax.all_to_all(pieces, "hz", 0, 0, tiled=False)
    return jnp.sum(pieces.astype(jnp.float32), axis=0)


def gather_over_head(value):
    value = lax.all_gather(value, "hz", axis=0, tiled=True)
    return lax.all_gather(value, "hx", axis=0, tiled=True)


def normalize_rows(layer_sum, mlp_gain):
    mean_square = jnp.mean(layer_sum * layer_sum, axis=1, keepdims=True)
    return (layer_sum * lax.rsqrt(mean_square + epsilon) * mlp_gain).astype(jnp.bfloat16)


def shards(
    x_in,
    z_in,
    bc,
    dt_raw,
    dt_bias,
    decay_rate,
    d_skip,
    norm_gain,
    out_weight,
    resid,
    mlp_gain,
    gate_weight,
    up_weight,
    down_weight,
):
    out_full, down_full = (
        lax.all_gather(out_weight, "seq", axis=1, tiled=True),
        lax.all_gather(down_weight, "seq", axis=1, tiled=True),
    )
    head_count = dt_raw.shape[0]
    length = dt_raw.shape[1]
    head_width = x_in.shape[1] // head_count
    step_size = jax.nn.softplus(dt_raw + dt_bias[:, None])
    log_decay = -decay_rate[:, None] * step_size
    x_heads = x_in.reshape(length, head_count, head_width)
    local_out, local_state = block_scan(x_heads, bc[0], bc[1], step_size, log_decay, BLOCK)
    running = jnp.cumsum(log_decay, axis=1)
    group_decay = jnp.exp(running[:, -1])
    entering = entering_state(group_decay, local_state)
    carried = jnp.einsum(
        "tn,hpn->thp", bc[1].astype(jnp.float32), entering, precision=lax.Precision.HIGHEST
    )
    carried = carried * jnp.exp(running).T[:, :, None]
    ssd_out = local_out + carried + d_skip[None, :, None] * x_heads.astype(jnp.float32)
    gated_out = ssd_out.reshape(length, head_count * head_width) * jax.nn.silu(
        z_in.astype(jnp.float32)
    )
    row_squares = jnp.sum(gated_out * gated_out, axis=1)
    gated_scaled = (gated_out * norm_gain).astype(jnp.bfloat16)
    head_n = lax.axis_size("hx") * lax.axis_size("hz")
    chunks = 1
    rows_per = length // head_n // chunks
    width = out_full.shape[1]
    gated_parts = gated_scaled.reshape(head_n, chunks, rows_per, -1)
    square_parts = row_squares.reshape(head_n, chunks, rows_per)
    resid_parts = resid.reshape(chunks, rows_per, -1)

    def packed_rows(chunk):
        chunk_rows = gated_parts[:, chunk].reshape(head_n * rows_per, -1)
        chunk_squares = square_parts[:, chunk].reshape(head_n * rows_per)
        partial_value = jnp.dot(chunk_rows, out_full, preferred_element_type=jnp.float32)
        sq_hi = chunk_squares.astype(jnp.bfloat16)
        sq_lo = (chunk_squares - sq_hi.astype(jnp.float32)).astype(jnp.bfloat16)
        extra = (
            jnp.zeros((head_n * rows_per, 128), jnp.bfloat16).at[:, 0].set(sq_hi).at[:, 1].set(sq_lo)
        )
        return jnp.concatenate([partial_value.astype(jnp.bfloat16), extra], axis=1)

    def finish_rows(reduced, chunk):
        part_rows = reduced[:, :width]
        part_squares = reduced[:, width] + reduced[:, width + 1]
        layer_sum = (
            resid_parts[chunk].astype(jnp.float32)
            + part_rows * lax.rsqrt(part_squares / INNER + epsilon)[:, None]
        )
        return layer_sum, normalize_rows(layer_sum, mlp_gain)

    def mlp_rows(rows_piece, down_full):
        gate_part = jnp.dot(rows_piece, gate_weight, preferred_element_type=jnp.float32)
        up_part = jnp.dot(rows_piece, up_weight, preferred_element_type=jnp.float32)
        hidden = (jax.nn.silu(gate_part) * up_part).astype(jnp.bfloat16)
        mlp_part = jnp.dot(hidden, down_full, preferred_element_type=jnp.float32)
        return sum_over_head(mlp_part.astype(jnp.bfloat16))

    packs = [packed_rows(chunk) for chunk in range(chunks)]
    normed_rows = []
    sums = []
    for chunk in range(chunks):
        pack = packs[chunk]
        if chunk > 0:
            pack, normed_rows[-1] = lax.optimization_barrier((pack, normed_rows[-1]))
        reduced = sum_over_head(pack)
        if chunk == 0:
            reduced, down_full = lax.optimization_barrier((reduced, down_full))
        layer_sum, normed = finish_rows(reduced, chunk)
        sums.append(layer_sum)
        normed_rows.append(normed)
    gathered = []
    for chunk in range(chunks):
        gathered.append(gather_over_head(normed_rows[chunk]))
        if chunk + 1 < chunks:
            gathered[-1], normed_rows[chunk + 1] = lax.optimization_barrier(
                (gathered[-1], normed_rows[chunk + 1])
            )
    outs = [sums[c] + mlp_rows(gathered[c], down_full) for c in range(chunks)]
    return jnp.concatenate(outs, axis=0).astype(jnp.bfloat16)


def solution(mesh):
    devices = mesh.devices.reshape(mesh.devices.shape[0], 4, mesh.devices.shape[1] // 4)
    mesh = jax.sharding.Mesh(devices, ("seq", "hx", "hz"))
    head = ("hx", "hz")
    in_specs = (
        P("seq", head),
        P("seq", head),
        P(None, "seq", None),
        P(head, "seq"),
        P(head),
        P(head),
        P(head),
        P(head),
        P(head, "seq"),
        P(("seq", "hx", "hz"), None),
        P(),
        P(None, head),
        P(None, head),
        P(head, "seq"),
    )
    out_specs = P(("seq", "hx", "hz"), None)
    return jax.shard_map(shards, mesh=mesh, in_specs=in_specs, out_specs=out_specs, check_vma=False)
```

```python
import jax
import jax.numpy as jnp
from jax import lax
from jax.sharding import PartitionSpec as P

BLOCK = 256
INNER = 8192


epsilon = 1e-05
SEQ = ("sy", "sz", "sc")


def block_scan(x_heads, b_rows, c_rows, step_size, log_decay, block_len):
    length, head_count, head_width = x_heads.shape
    state_size = b_rows.shape[1]
    block_count = length // block_len
    lower_mask = jnp.tril(jnp.ones((block_len, block_len), dtype=bool))
    carry_state = jnp.zeros((head_count, head_width, state_size), jnp.float32)
    outs = []
    for blk in range(block_count):
        rows = slice(blk * block_len, (blk + 1) * block_len)
        x_block = x_heads[rows]
        b_block = b_rows[rows]
        c_block = c_rows[rows]
        d_block = step_size[:, rows]
        a_block = log_decay[:, rows]
        cumulative = jnp.cumsum(a_block, axis=1)
        gap_values = jnp.where(
            lower_mask[None], cumulative[:, :, None] - cumulative[:, None, :], -jnp.inf
        )
        scores = jnp.dot(c_block, b_block.T, preferred_element_type=jnp.float32)
        mixing = (jnp.exp(gap_values) * scores[None] * d_block[:, None, :]).astype(jnp.bfloat16)
        within = jnp.einsum("hij,jhp->ihp", mixing, x_block, preferred_element_type=jnp.float32)
        if blk > 0:
            carried = jnp.einsum(
                "in,hpn->ihp", c_block.astype(jnp.float32), carry_state,
                precision=lax.Precision.HIGHEST,
            )
            within = within + carried * jnp.exp(cumulative).T[:, :, None]
        last_cum = cumulative[:, -1:]
        inject = (
            (jnp.exp(last_cum - cumulative) * d_block)[:, :, None]
            * b_block.astype(jnp.float32)[None]
        ).astype(jnp.bfloat16)
        added = jnp.einsum("jhp,hjn->hpn", x_block, inject, preferred_element_type=jnp.float32)
        carry_state = jnp.exp(last_cum)[:, :, None] * carry_state + added
        outs.append(within)
    return jnp.concatenate(outs, axis=0), carry_state


def combine(first, second):
    (d1, s1), (d2, s2) = first, second
    return d1 * d2, d2[:, None, None] * s1 + s2


def send(pair, pairs, axes):
    return tuple(lax.ppermute(v, axes, pairs) for v in pair)


def entering_state(group_decay, local_state):
    block = ("sz", "sc")
    j = lax.axis_index("sz") * 2 + lax.axis_index("sc")
    y = lax.axis_index("sy")
    ny = lax.axis_size("sy")
    own = (group_decay, local_state)
    ident = (jnp.ones_like(group_decay), jnp.zeros_like(local_state))

    def pick(cond, a, b):
        return tuple(jnp.where(cond, u, v) for u, v in zip(a, b))

    got = send(own, [(0, 1), (2, 3)], block)
    pair_agg = combine(got, own)
    lower = send(pair_agg, [(1, 2)], block)
    lower3 = send(lower, [(2, 3)], block)
    inner = pick(j == 1, got, ident)
    inner = pick(j == 2, lower, inner)
    inner = pick(j == 3, combine(lower3, got), inner)
    block_agg = combine(lower3, pair_agg)
    full = SEQ
    before = ident
    for k in range(ny - 1, 0, -1):
        pairs = [(4 * src + 3, 4 * (src + k) + 3) for src in range(ny - k)]
        got_k = send(block_agg, pairs, full)
        before = combine(before, pick(y >= k, got_k, ident))
    to_2 = send(before, [(3, 2)], block)
    to_1 = send(before, [(3, 1)], block)
    to_0 = send(to_1, [(1, 0)], block)
    prefix = pick(j == 3, before, to_0)
    prefix = pick(j == 2, to_2, prefix)
    prefix = pick(j == 1, to_1, prefix)
    return combine(prefix, inner)[1]


def sum_over_head(value):
    nx, nz = lax.axis_size("hx"), lax.axis_size("hz")
    pieces = value.reshape(nx, nz, value.shape[0] // (nx * nz), value.shape[1])
    pieces = lax.all_to_all(pieces, "hx", 0, 0, tiled=False)
    pieces = jnp.sum(pieces.astype(jnp.float32), axis=0).astype(jnp.bfloat16)
    pieces = lax.all_to_all(pieces, "hz", 0, 0, tiled=False)
    return jnp.sum(pieces.astype(jnp.float32), axis=0)


def gather_over_head(value):
    value = lax.all_gather(value, "hz", axis=0, tiled=True)
    return lax.all_gather(value, "hx", axis=0, tiled=True)


def normalize_rows(layer_sum, mlp_gain):
    mean_square = jnp.mean(layer_sum * layer_sum, axis=1, keepdims=True)
    return (layer_sum * lax.rsqrt(mean_square + epsilon) * mlp_gain).astype(jnp.bfloat16)


def shards(
    x_in,
    z_in,
    bc,
    dt_raw,
    dt_bias,
    decay_rate,
    d_skip,
    norm_gain,
    out_weight,
    resid,
    mlp_gain,
    gate_weight,
    up_weight,
    down_weight,
):
    out_full, down_full = (
        lax.all_gather(out_weight, SEQ, axis=1, tiled=True),
        lax.all_gather(down_weight, SEQ, axis=1, tiled=True),
    )
    head_count = dt_raw.shape[0]
    length = dt_raw.shape[1]
    head_width = x_in.shape[1] // head_count
    step_size = jax.nn.softplus(dt_raw + dt_bias[:, None])
    log_decay = -decay_rate[:, None] * step_size
    x_heads = x_in.reshape(length, head_count, head_width)
    local_out, local_state = block_scan(x_heads, bc[0], bc[1], step_size, log_decay, BLOCK)
    running = jnp.cumsum(log_decay, axis=1)
    group_decay = jnp.exp(running[:, -1])
    entering = entering_state(group_decay, local_state)
    carried = jnp.einsum(
        "tn,hpn->thp", bc[1].astype(jnp.float32), entering, precision=lax.Precision.HIGHEST
    )
    carried = carried * jnp.exp(running).T[:, :, None]
    ssd_out = local_out + carried + d_skip[None, :, None] * x_heads.astype(jnp.float32)
    gated_out = ssd_out.reshape(length, head_count * head_width) * jax.nn.silu(
        z_in.astype(jnp.float32)
    )
    row_squares = jnp.sum(gated_out * gated_out, axis=1)
    gated_scaled = (gated_out * norm_gain).astype(jnp.bfloat16)
    head_n = lax.axis_size("hx") * lax.axis_size("hz")
    chunks = 1
    rows_per = length // head_n // chunks
    width = out_full.shape[1]
    gated_parts = gated_scaled.reshape(head_n, chunks, rows_per, -1)
    square_parts = row_squares.reshape(head_n, chunks, rows_per)
    resid_parts = resid.reshape(chunks, rows_per, -1)

    def packed_rows(chunk):
        chunk_rows = gated_parts[:, chunk].reshape(head_n * rows_per, -1)
        chunk_squares = square_parts[:, chunk].reshape(head_n * rows_per)
        partial_value = jnp.dot(chunk_rows, out_full, preferred_element_type=jnp.float32)
        sq_hi = chunk_squares.astype(jnp.bfloat16)
        sq_lo = (chunk_squares - sq_hi.astype(jnp.float32)).astype(jnp.bfloat16)
        extra = (
            jnp.zeros((head_n * rows_per, 128), jnp.bfloat16).at[:, 0].set(sq_hi).at[:, 1].set(sq_lo)
        )
        return jnp.concatenate([partial_value.astype(jnp.bfloat16), extra], axis=1)

    def finish_rows(reduced, chunk):
        part_rows = reduced[:, :width]
        part_squares = reduced[:, width] + reduced[:, width + 1]
        layer_sum = (
            resid_parts[chunk].astype(jnp.float32)
            + part_rows * lax.rsqrt(part_squares / INNER + epsilon)[:, None]
        )
        return layer_sum, normalize_rows(layer_sum, mlp_gain)

    def mlp_rows(rows_piece, down_full):
        gate_part = jnp.dot(rows_piece, gate_weight, preferred_element_type=jnp.float32)
        up_part = jnp.dot(rows_piece, up_weight, preferred_element_type=jnp.float32)
        hidden = (jax.nn.silu(gate_part) * up_part).astype(jnp.bfloat16)
        mlp_part = jnp.dot(hidden, down_full, preferred_element_type=jnp.float32)
        return sum_over_head(mlp_part.astype(jnp.bfloat16))

    packs = [packed_rows(chunk) for chunk in range(chunks)]
    normed_rows = []
    sums = []
    for chunk in range(chunks):
        pack = packs[chunk]
        if chunk > 0:
            pack, normed_rows[-1] = lax.optimization_barrier((pack, normed_rows[-1]))
        reduced = sum_over_head(pack)
        if chunk == 0:
            reduced, down_full = lax.optimization_barrier((reduced, down_full))
        layer_sum, normed = finish_rows(reduced, chunk)
        sums.append(layer_sum)
        normed_rows.append(normed)
    gathered = []
    for chunk in range(chunks):
        gathered.append(gather_over_head(normed_rows[chunk]))
        if chunk + 1 < chunks:
            gathered[-1], normed_rows[chunk + 1] = lax.optimization_barrier(
                (gathered[-1], normed_rows[chunk + 1])
            )
    outs = [sums[c] + mlp_rows(gathered[c], down_full) for c in range(chunks)]
    return jnp.concatenate(outs, axis=0).astype(jnp.bfloat16)


def solution(mesh):
    seq_n, head_n = mesh.devices.shape
    devices = mesh.devices.reshape(seq_n // 4, 2, 2, 4, head_n // 4)
    mesh = jax.sharding.Mesh(devices, ("sy", "sz", "sc", "hx", "hz"))
    head = ("hx", "hz")
    in_specs = (
        P(SEQ, head),
        P(SEQ, head),
        P(None, SEQ, None),
        P(head, SEQ),
        P(head),
        P(head),
        P(head),
        P(head),
        P(head, SEQ),
        P(SEQ + head, None),
        P(),
        P(None, head),
        P(None, head),
        P(head, SEQ),
    )
    out_specs = P(SEQ + head, None)
    return jax.shard_map(shards, mesh=mesh, in_specs=in_specs, out_specs=out_specs, check_vma=False)
```

```python
import jax
import jax.numpy as jnp
from jax import lax
from jax.sharding import PartitionSpec as P

BLOCK = 256
INNER = 8192


epsilon = 1e-05
SEQ = ("sy", "sz", "sc")


def block_scan(x_heads, b_rows, c_rows, step_size, log_decay, block_len):
    length, head_count, head_width = x_heads.shape
    state_size = b_rows.shape[1]
    block_count = length // block_len
    lower_mask = jnp.tril(jnp.ones((block_len, block_len), dtype=bool))
    carry_state = jnp.zeros((head_count, head_width, state_size), jnp.float32)
    outs = []
    for blk in range(block_count):
        rows = slice(blk * block_len, (blk + 1) * block_len)
        x_block = x_heads[rows]
        b_block = b_rows[rows]
        c_block = c_rows[rows]
        d_block = step_size[:, rows]
        a_block = log_decay[:, rows]
        cumulative = jnp.cumsum(a_block, axis=1)
        gap_values = jnp.where(
            lower_mask[None], cumulative[:, :, None] - cumulative[:, None, :], -jnp.inf
        )
        scores = jnp.dot(c_block, b_block.T, preferred_element_type=jnp.float32)
        mixing = (jnp.exp(gap_values) * scores[None] * d_block[:, None, :]).astype(jnp.bfloat16)
        within = jnp.einsum("hij,jhp->ihp", mixing, x_block, preferred_element_type=jnp.float32)
        if blk > 0:
            carried = jnp.einsum(
                "in,hpn->ihp", c_block.astype(jnp.float32), carry_state,
                precision=lax.Precision.HIGHEST,
            )
            within = within + carried * jnp.exp(cumulative).T[:, :, None]
        last_cum = cumulative[:, -1:]
        inject = (
            (jnp.exp(last_cum - cumulative) * d_block)[:, :, None]
            * b_block.astype(jnp.float32)[None]
        ).astype(jnp.bfloat16)
        added = jnp.einsum("jhp,hjn->hpn", x_block, inject, preferred_element_type=jnp.float32)
        carry_state = jnp.exp(last_cum)[:, :, None] * carry_state + added
        outs.append(within)
    return jnp.concatenate(outs, axis=0), carry_state


def combine(first, second):
    (d1, s1), (d2, s2) = first, second
    return d1 * d2, d2[:, None, None] * s1 + s2


def send(pair, pairs, axes):
    return tuple(lax.ppermute(v, axes, pairs) for v in pair)


def entering_state(group_decay, local_state):
    block = ("sz", "sc")
    j = lax.axis_index("sz") * 2 + lax.axis_index("sc")
    y = lax.axis_index("sy")
    ny = lax.axis_size("sy")
    own = (group_decay, local_state)
    ident = (jnp.ones_like(group_decay), jnp.zeros_like(local_state))

    def pick(cond, a, b):
        return tuple(jnp.where(cond, u, v) for u, v in zip(a, b))

    got = send(own, [(0, 1), (2, 3)], block)
    pair_agg = combine(got, own)
    lower = send(pair_agg, [(1, 2)], block)
    lower3 = send(lower, [(2, 3)], block)
    inner = pick(j == 1, got, ident)
    inner = pick(j == 2, lower, inner)
    inner = pick(j == 3, combine(lower3, got), inner)
    block_agg = combine(lower3, pair_agg)
    full = SEQ
    before = ident
    for k in range(ny - 1, 0, -1):
        pairs = [(4 * src + 3, 4 * (src + k) + 3) for src in range(ny - k)]
        got_k = send(block_agg, pairs, full)
        before = combine(before, pick(y >= k, got_k, ident))
    to_2 = send(before, [(3, 2)], block)
    to_1 = send(before, [(3, 1)], block)
    to_0 = send(to_1, [(1, 0)], block)
    prefix = pick(j == 3, before, to_0)
    prefix = pick(j == 2, to_2, prefix)
    prefix = pick(j == 1, to_1, prefix)
    return combine(prefix, inner)[1]


def ring_sum_x(pieces):
    nx = pieces.shape[0]
    x = lax.axis_index("hx")
    half = pieces.shape[2] // 2
    ways = ((1, pieces[:, :, :half]), (-1, pieces[:, :, half:]))
    accs = []
    for way, part in ways:
        pairs = [(src, (src + way) % nx) for src in range(nx)]
        acc = jnp.take(part, (x - way) % nx, axis=0).astype(jnp.float32)
        for step in range(nx - 1):
            got = lax.ppermute(acc.astype(jnp.bfloat16), "hx", pairs)
            chunk = (x - way * (step + 2)) % nx
            acc = got.astype(jnp.float32) + jnp.take(part, chunk, axis=0).astype(jnp.float32)
        accs.append(acc)
    return jnp.concatenate(accs, axis=1)


def sum_over_head(value):
    nx, nz = lax.axis_size("hx"), lax.axis_size("hz")
    pieces = value.reshape(nx, nz, value.shape[0] // (nx * nz), value.shape[1])
    pieces = ring_sum_x(pieces).astype(jnp.bfloat16)
    pieces = lax.all_to_all(pieces, "hz", 0, 0, tiled=False)
    return jnp.sum(pieces.astype(jnp.float32), axis=0)


def gather_over_head(value):
    value = lax.all_gather(value, "hz", axis=0, tiled=True)
    return lax.all_gather(value, "hx", axis=0, tiled=True)


def normalize_rows(layer_sum, mlp_gain):
    mean_square = jnp.mean(layer_sum * layer_sum, axis=1, keepdims=True)
    return (layer_sum * lax.rsqrt(mean_square + epsilon) * mlp_gain).astype(jnp.bfloat16)


def shards(
    x_in,
    z_in,
    bc,
    dt_raw,
    dt_bias,
    decay_rate,
    d_skip,
    norm_gain,
    out_weight,
    resid,
    mlp_gain,
    gate_weight,
    up_weight,
    down_weight,
):
    out_full, down_full = (
        lax.all_gather(out_weight, SEQ, axis=1, tiled=True),
        lax.all_gather(down_weight, SEQ, axis=1, tiled=True),
    )
    head_count = dt_raw.shape[0]
    length = dt_raw.shape[1]
    head_width = x_in.shape[1] // head_count
    step_size = jax.nn.softplus(dt_raw + dt_bias[:, None])
    log_decay = -decay_rate[:, None] * step_size
    x_heads = x_in.reshape(length, head_count, head_width)
    local_out, local_state = block_scan(x_heads, bc[0], bc[1], step_size, log_decay, BLOCK)
    running = jnp.cumsum(log_decay, axis=1)
    group_decay = jnp.exp(running[:, -1])
    entering = entering_state(group_decay, local_state)
    carried = jnp.einsum(
        "tn,hpn->thp", bc[1].astype(jnp.float32), entering, precision=lax.Precision.HIGHEST
    )
    carried = carried * jnp.exp(running).T[:, :, None]
    ssd_out = local_out + carried + d_skip[None, :, None] * x_heads.astype(jnp.float32)
    gated_out = ssd_out.reshape(length, head_count * head_width) * jax.nn.silu(
        z_in.astype(jnp.float32)
    )
    row_squares = jnp.sum(gated_out * gated_out, axis=1)
    gated_scaled = (gated_out * norm_gain).astype(jnp.bfloat16)
    head_n = lax.axis_size("hx") * lax.axis_size("hz")
    chunks = 1
    rows_per = length // head_n // chunks
    width = out_full.shape[1]
    gated_parts = gated_scaled.reshape(head_n, chunks, rows_per, -1)
    square_parts = row_squares.reshape(head_n, chunks, rows_per)
    resid_parts = resid.reshape(chunks, rows_per, -1)

    def packed_rows(chunk):
        chunk_rows = gated_parts[:, chunk].reshape(head_n * rows_per, -1)
        chunk_squares = square_parts[:, chunk].reshape(head_n * rows_per)
        partial_value = jnp.dot(chunk_rows, out_full, preferred_element_type=jnp.float32)
        sq_hi = chunk_squares.astype(jnp.bfloat16)
        sq_lo = (chunk_squares - sq_hi.astype(jnp.float32)).astype(jnp.bfloat16)
        extra = (
            jnp.zeros((head_n * rows_per, 128), jnp.bfloat16).at[:, 0].set(sq_hi).at[:, 1].set(sq_lo)
        )
        return jnp.concatenate([partial_value.astype(jnp.bfloat16), extra], axis=1)

    def finish_rows(reduced, chunk):
        part_rows = reduced[:, :width]
        part_squares = reduced[:, width] + reduced[:, width + 1]
        layer_sum = (
            resid_parts[chunk].astype(jnp.float32)
            + part_rows * lax.rsqrt(part_squares / INNER + epsilon)[:, None]
        )
        return layer_sum, normalize_rows(layer_sum, mlp_gain)

    def mlp_rows(rows_piece, down_full):
        gate_part = jnp.dot(rows_piece, gate_weight, preferred_element_type=jnp.float32)
        up_part = jnp.dot(rows_piece, up_weight, preferred_element_type=jnp.float32)
        hidden = (jax.nn.silu(gate_part) * up_part).astype(jnp.bfloat16)
        mlp_part = jnp.dot(hidden, down_full, preferred_element_type=jnp.float32)
        return sum_over_head(mlp_part.astype(jnp.bfloat16))

    packs = [packed_rows(chunk) for chunk in range(chunks)]
    normed_rows = []
    sums = []
    for chunk in range(chunks):
        pack = packs[chunk]
        if chunk > 0:
            pack, normed_rows[-1] = lax.optimization_barrier((pack, normed_rows[-1]))
        reduced = sum_over_head(pack)
        if chunk == 0:
            reduced, down_full = lax.optimization_barrier((reduced, down_full))
        layer_sum, normed = finish_rows(reduced, chunk)
        sums.append(layer_sum)
        normed_rows.append(normed)
    gathered = []
    for chunk in range(chunks):
        gathered.append(gather_over_head(normed_rows[chunk]))
        if chunk + 1 < chunks:
            gathered[-1], normed_rows[chunk + 1] = lax.optimization_barrier(
                (gathered[-1], normed_rows[chunk + 1])
            )
    outs = [sums[c] + mlp_rows(gathered[c], down_full) for c in range(chunks)]
    return jnp.concatenate(outs, axis=0).astype(jnp.bfloat16)


def solution(mesh):
    seq_n, head_n = mesh.devices.shape
    devices = mesh.devices.reshape(seq_n // 4, 2, 2, 4, head_n // 4)
    mesh = jax.sharding.Mesh(devices, ("sy", "sz", "sc", "hx", "hz"))
    head = ("hx", "hz")
    in_specs = (
        P(SEQ, head),
        P(SEQ, head),
        P(None, SEQ, None),
        P(head, SEQ),
        P(head),
        P(head),
        P(head),
        P(head),
        P(head, SEQ),
        P(SEQ + head, None),
        P(),
        P(None, head),
        P(None, head),
        P(head, SEQ),
    )
    out_specs = P(SEQ + head, None)
    return jax.shard_map(shards, mesh=mesh, in_specs=in_specs, out_specs=out_specs, check_vma=False)
```

```python
import jax
import jax.numpy as jnp
from jax import lax
from jax.sharding import PartitionSpec as P

BLOCK = 256
INNER = 8192


epsilon = 1e-05
SEQ = ("sy", "sz", "sc")


def block_scan(x_heads, b_rows, c_rows, step_size, log_decay, block_len):
    length, head_count, head_width = x_heads.shape
    state_size = b_rows.shape[1]
    block_count = length // block_len
    lower_mask = jnp.tril(jnp.ones((block_len, block_len), dtype=bool))
    carry_state = jnp.zeros((head_count, head_width, state_size), jnp.float32)
    outs = []
    for blk in range(block_count):
        rows = slice(blk * block_len, (blk + 1) * block_len)
        x_block = x_heads[rows]
        b_block = b_rows[rows]
        c_block = c_rows[rows]
        d_block = step_size[:, rows]
        a_block = log_decay[:, rows]
        cumulative = jnp.cumsum(a_block, axis=1)
        gap_values = jnp.where(
            lower_mask[None], cumulative[:, :, None] - cumulative[:, None, :], -jnp.inf
        )
        scores = jnp.dot(c_block, b_block.T, preferred_element_type=jnp.float32)
        mixing = (jnp.exp(gap_values) * scores[None] * d_block[:, None, :]).astype(jnp.bfloat16)
        within = jnp.einsum("hij,jhp->ihp", mixing, x_block, preferred_element_type=jnp.float32)
        if blk > 0:
            carried = jnp.einsum(
                "in,hpn->ihp", c_block.astype(jnp.float32), carry_state,
                precision=lax.Precision.HIGHEST,
            )
            within = within + carried * jnp.exp(cumulative).T[:, :, None]
        last_cum = cumulative[:, -1:]
        inject = (
            (jnp.exp(last_cum - cumulative) * d_block)[:, :, None]
            * b_block.astype(jnp.float32)[None]
        ).astype(jnp.bfloat16)
        added = jnp.einsum("jhp,hjn->hpn", x_block, inject, preferred_element_type=jnp.float32)
        carry_state = jnp.exp(last_cum)[:, :, None] * carry_state + added
        outs.append(within)
    return jnp.concatenate(outs, axis=0), carry_state


def combine(first, second):
    (d1, s1), (d2, s2) = first, second
    return d1 * d2, d2[:, None, None] * s1 + s2


def send(pair, pairs, axes):
    return tuple(lax.ppermute(v, axes, pairs) for v in pair)


def entering_state(group_decay, local_state):
    block = ("sz", "sc")
    j = lax.axis_index("sz") * 2 + lax.axis_index("sc")
    y = lax.axis_index("sy")
    ny = lax.axis_size("sy")
    own = (group_decay, local_state)
    ident = (jnp.ones_like(group_decay), jnp.zeros_like(local_state))

    def pick(cond, a, b):
        return tuple(jnp.where(cond, u, v) for u, v in zip(a, b))

    got = send(own, [(0, 1), (2, 3)], block)
    pair_agg = combine(got, own)
    lower = send(pair_agg, [(1, 2)], block)
    lower3 = send(lower, [(2, 3)], block)
    inner = pick(j == 1, got, ident)
    inner = pick(j == 2, lower, inner)
    inner = pick(j == 3, combine(lower3, got), inner)
    block_agg = combine(lower3, pair_agg)
    full = SEQ
    before = ident
    for k in range(ny - 1, 0, -1):
        pairs = [(4 * src + 3, 4 * (src + k) + 3) for src in range(ny - k)]
        got_k = send(block_agg, pairs, full)
        before = combine(before, pick(y >= k, got_k, ident))
    to_2 = send(before, [(3, 2)], block)
    to_1 = send(before, [(3, 1)], block)
    to_0 = send(to_1, [(1, 0)], block)
    prefix = pick(j == 3, before, to_0)
    prefix = pick(j == 2, to_2, prefix)
    prefix = pick(j == 1, to_1, prefix)
    return combine(prefix, inner)[1]


def ring_sum_x(pieces):
    nx = pieces.shape[0]
    x = lax.axis_index("hx")
    half = pieces.shape[2] // 2
    ways = ((1, pieces[:, :, :half]), (-1, pieces[:, :, half:]))
    accs = []
    for way, part in ways:
        pairs = [(src, (src + way) % nx) for src in range(nx)]
        acc = jnp.take(part, (x - way) % nx, axis=0).astype(jnp.float32)
        for step in range(nx - 1):
            got = lax.ppermute(acc.astype(jnp.bfloat16), "hx", pairs)
            chunk = (x - way * (step + 2)) % nx
            acc = got.astype(jnp.float32) + jnp.take(part, chunk, axis=0).astype(jnp.float32)
        accs.append(acc)
    return jnp.concatenate(accs, axis=1)


def sum_over_head(value):
    nx, nz = lax.axis_size("hx"), lax.axis_size("hz")
    pieces = value.reshape(nx, nz, value.shape[0] // (nx * nz), value.shape[1])
    pieces = ring_sum_x(pieces).astype(jnp.bfloat16)
    pieces = lax.all_to_all(pieces, "hz", 0, 0, tiled=False)
    return jnp.sum(pieces.astype(jnp.float32), axis=0)


def ring_gather_x(value):
    nx = lax.axis_size("hx")
    x = lax.axis_index("hx")
    half = value.shape[0] // 2
    slots = jnp.arange(nx)
    outs = []
    for way, part in ((1, value[:half]), (-1, value[half:])):
        pairs = [(src, (src + way) % nx) for src in range(nx)]
        got = [part]
        for step in range(nx - 1):
            got.append(lax.ppermute(got[-1], "hx", pairs))
        stacked = jnp.stack(got)
        outs.append(jnp.take(stacked, (way * (x - slots)) % nx, axis=0))
    return jnp.concatenate(outs, axis=1).reshape(nx * value.shape[0], value.shape[1])


def gather_over_head(value):
    value = lax.all_gather(value, "hz", axis=0, tiled=True)
    return ring_gather_x(value)


def normalize_rows(layer_sum, mlp_gain):
    mean_square = jnp.mean(layer_sum * layer_sum, axis=1, keepdims=True)
    return (layer_sum * lax.rsqrt(mean_square + epsilon) * mlp_gain).astype(jnp.bfloat16)


def shards(
    x_in,
    z_in,
    bc,
    dt_raw,
    dt_bias,
    decay_rate,
    d_skip,
    norm_gain,
    out_weight,
    resid,
    mlp_gain,
    gate_weight,
    up_weight,
    down_weight,
):
    out_full, down_full = (
        lax.all_gather(out_weight, SEQ, axis=1, tiled=True),
        lax.all_gather(down_weight, SEQ, axis=1, tiled=True),
    )
    head_count = dt_raw.shape[0]
    length = dt_raw.shape[1]
    head_width = x_in.shape[1] // head_count
    step_size = jax.nn.softplus(dt_raw + dt_bias[:, None])
    log_decay = -decay_rate[:, None] * step_size
    x_heads = x_in.reshape(length, head_count, head_width)
    local_out, local_state = block_scan(x_heads, bc[0], bc[1], step_size, log_decay, BLOCK)
    running = jnp.cumsum(log_decay, axis=1)
    group_decay = jnp.exp(running[:, -1])
    entering = entering_state(group_decay, local_state)
    carried = jnp.einsum(
        "tn,hpn->thp", bc[1].astype(jnp.float32), entering, precision=lax.Precision.HIGHEST
    )
    carried = carried * jnp.exp(running).T[:, :, None]
    ssd_out = local_out + carried + d_skip[None, :, None] * x_heads.astype(jnp.float32)
    gated_out = ssd_out.reshape(length, head_count * head_width) * jax.nn.silu(
        z_in.astype(jnp.float32)
    )
    row_squares = jnp.sum(gated_out * gated_out, axis=1)
    gated_scaled = (gated_out * norm_gain).astype(jnp.bfloat16)
    head_n = lax.axis_size("hx") * lax.axis_size("hz")
    chunks = 1
    rows_per = length // head_n // chunks
    width = out_full.shape[1]
    gated_parts = gated_scaled.reshape(head_n, chunks, rows_per, -1)
    square_parts = row_squares.reshape(head_n, chunks, rows_per)
    resid_parts = resid.reshape(chunks, rows_per, -1)

    def packed_rows(chunk):
        chunk_rows = gated_parts[:, chunk].reshape(head_n * rows_per, -1)
        chunk_squares = square_parts[:, chunk].reshape(head_n * rows_per)
        partial_value = jnp.dot(chunk_rows, out_full, preferred_element_type=jnp.float32)
        sq_hi = chunk_squares.astype(jnp.bfloat16)
        sq_lo = (chunk_squares - sq_hi.astype(jnp.float32)).astype(jnp.bfloat16)
        extra = (
            jnp.zeros((head_n * rows_per, 128), jnp.bfloat16).at[:, 0].set(sq_hi).at[:, 1].set(sq_lo)
        )
        return jnp.concatenate([partial_value.astype(jnp.bfloat16), extra], axis=1)

    def finish_rows(reduced, chunk):
        part_rows = reduced[:, :width]
        part_squares = reduced[:, width] + reduced[:, width + 1]
        layer_sum = (
            resid_parts[chunk].astype(jnp.float32)
            + part_rows * lax.rsqrt(part_squares / INNER + epsilon)[:, None]
        )
        return layer_sum, normalize_rows(layer_sum, mlp_gain)

    def mlp_rows(rows_piece, down_full):
        gate_part = jnp.dot(rows_piece, gate_weight, preferred_element_type=jnp.float32)
        up_part = jnp.dot(rows_piece, up_weight, preferred_element_type=jnp.float32)
        hidden = (jax.nn.silu(gate_part) * up_part).astype(jnp.bfloat16)
        mlp_part = jnp.dot(hidden, down_full, preferred_element_type=jnp.float32)
        return sum_over_head(mlp_part.astype(jnp.bfloat16))

    packs = [packed_rows(chunk) for chunk in range(chunks)]
    normed_rows = []
    sums = []
    for chunk in range(chunks):
        pack = packs[chunk]
        if chunk > 0:
            pack, normed_rows[-1] = lax.optimization_barrier((pack, normed_rows[-1]))
        reduced = sum_over_head(pack)
        if chunk == 0:
            reduced, down_full = lax.optimization_barrier((reduced, down_full))
        layer_sum, normed = finish_rows(reduced, chunk)
        sums.append(layer_sum)
        normed_rows.append(normed)
    gathered = []
    for chunk in range(chunks):
        gathered.append(gather_over_head(normed_rows[chunk]))
        if chunk + 1 < chunks:
            gathered[-1], normed_rows[chunk + 1] = lax.optimization_barrier(
                (gathered[-1], normed_rows[chunk + 1])
            )
    outs = [sums[c] + mlp_rows(gathered[c], down_full) for c in range(chunks)]
    return jnp.concatenate(outs, axis=0).astype(jnp.bfloat16)


def solution(mesh):
    seq_n, head_n = mesh.devices.shape
    devices = mesh.devices.reshape(seq_n // 4, 2, 2, 4, head_n // 4)
    mesh = jax.sharding.Mesh(devices, ("sy", "sz", "sc", "hx", "hz"))
    head = ("hx", "hz")
    in_specs = (
        P(SEQ, head),
        P(SEQ, head),
        P(None, SEQ, None),
        P(head, SEQ),
        P(head),
        P(head),
        P(head),
        P(head),
        P(head, SEQ),
        P(SEQ + head, None),
        P(),
        P(None, head),
        P(None, head),
        P(head, SEQ),
    )
    out_specs = P(SEQ + head, None)
    return jax.shard_map(shards, mesh=mesh, in_specs=in_specs, out_specs=out_specs, check_vma=False)
```

```python
import jax
import jax.numpy as jnp
from jax import lax
from jax.sharding import PartitionSpec as P

BLOCK = 256
INNER = 8192


epsilon = 1e-05
SEQ = ("sy", "sz", "sc")


def block_scan(x_heads, b_rows, c_rows, step_size, log_decay, block_len):
    length, head_count, head_width = x_heads.shape
    state_size = b_rows.shape[1]
    block_count = length // block_len
    lower_mask = jnp.tril(jnp.ones((block_len, block_len), dtype=bool))
    carry_state = jnp.zeros((head_count, head_width, state_size), jnp.float32)
    outs = []
    for blk in range(block_count):
        rows = slice(blk * block_len, (blk + 1) * block_len)
        x_block = x_heads[rows]
        b_block = b_rows[rows]
        c_block = c_rows[rows]
        d_block = step_size[:, rows]
        a_block = log_decay[:, rows]
        cumulative = jnp.cumsum(a_block, axis=1)
        gap_values = jnp.where(
            lower_mask[None], cumulative[:, :, None] - cumulative[:, None, :], -jnp.inf
        )
        scores = jnp.dot(c_block, b_block.T, preferred_element_type=jnp.float32)
        mixing = (jnp.exp(gap_values) * scores[None] * d_block[:, None, :]).astype(jnp.bfloat16)
        within = jnp.einsum("hij,jhp->ihp", mixing, x_block, preferred_element_type=jnp.float32)
        if blk > 0:
            carried = jnp.einsum(
                "in,hpn->ihp", c_block.astype(jnp.float32), carry_state,
                precision=lax.Precision.HIGHEST,
            )
            within = within + carried * jnp.exp(cumulative).T[:, :, None]
        last_cum = cumulative[:, -1:]
        inject = (
            (jnp.exp(last_cum - cumulative) * d_block)[:, :, None]
            * b_block.astype(jnp.float32)[None]
        ).astype(jnp.bfloat16)
        added = jnp.einsum("jhp,hjn->hpn", x_block, inject, preferred_element_type=jnp.float32)
        carry_state = jnp.exp(last_cum)[:, :, None] * carry_state + added
        outs.append(within)
    return jnp.concatenate(outs, axis=0), carry_state


def combine(first, second):
    (d1, s1), (d2, s2) = first, second
    return d1 * d2, d2[:, None, None] * s1 + s2


def send(pair, pairs, axes):
    return tuple(lax.ppermute(v, axes, pairs) for v in pair)


def entering_state(group_decay, local_state):
    block = ("sz", "sc")
    j = lax.axis_index("sz") * 2 + lax.axis_index("sc")
    y = lax.axis_index("sy")
    ny = lax.axis_size("sy")
    own = (group_decay, local_state)
    ident = (jnp.ones_like(group_decay), jnp.zeros_like(local_state))

    def pick(cond, a, b):
        return tuple(jnp.where(cond, u, v) for u, v in zip(a, b))

    got = send(own, [(0, 1), (2, 3)], block)
    pair_agg = combine(got, own)
    lower = send(pair_agg, [(1, 2)], block)
    lower3 = send(lower, [(2, 3)], block)
    inner = pick(j == 1, got, ident)
    inner = pick(j == 2, lower, inner)
    inner = pick(j == 3, combine(lower3, got), inner)
    block_agg = combine(lower3, pair_agg)
    full = SEQ
    before = ident
    for k in range(ny - 1, 0, -1):
        pairs = [(4 * src + 3, 4 * (src + k) + 3) for src in range(ny - k)]
        got_k = send(block_agg, pairs, full)
        before = combine(before, pick(y >= k, got_k, ident))
    to_2 = send(before, [(3, 2)], block)
    to_1 = send(before, [(3, 1)], block)
    to_0 = send(to_1, [(1, 0)], block)
    prefix = pick(j == 3, before, to_0)
    prefix = pick(j == 2, to_2, prefix)
    prefix = pick(j == 1, to_1, prefix)
    return combine(prefix, inner)[1]


def ring_sum_x(pieces):
    nx = pieces.shape[0]
    x = lax.axis_index("hx")
    half = pieces.shape[2] // 2
    ways = ((1, pieces[:, :, :half]), (-1, pieces[:, :, half:]))
    accs = []
    for way, part in ways:
        pairs = [(src, (src + way) % nx) for src in range(nx)]
        acc = jnp.take(part, (x - way) % nx, axis=0).astype(jnp.float32)
        for step in range(nx - 1):
            got = lax.ppermute(acc.astype(jnp.bfloat16), "hx", pairs)
            chunk = (x - way * (step + 2)) % nx
            acc = got.astype(jnp.float32) + jnp.take(part, chunk, axis=0).astype(jnp.float32)
        accs.append(acc)
    return jnp.concatenate(accs, axis=1)


def sum_over_head(value):
    nx, nz = lax.axis_size("hx"), lax.axis_size("hz")
    pieces = value.reshape(nx, nz, value.shape[0] // (nx * nz), value.shape[1])
    pieces = ring_sum_x(pieces).astype(jnp.bfloat16)
    pieces = lax.all_to_all(pieces, "hz", 0, 0, tiled=False)
    return jnp.sum(pieces.astype(jnp.float32), axis=0)


def ring_gather_x(value):
    nx = lax.axis_size("hx")
    x = lax.axis_index("hx")
    half = value.shape[0] // 2
    slots = jnp.arange(nx)
    outs = []
    for way, part in ((1, value[:half]), (-1, value[half:])):
        pairs = [(src, (src + way) % nx) for src in range(nx)]
        got = [part]
        for step in range(nx - 1):
            got.append(lax.ppermute(got[-1], "hx", pairs))
        stacked = jnp.stack(got)
        outs.append(jnp.take(stacked, (way * (x - slots)) % nx, axis=0))
    return jnp.concatenate(outs, axis=1).reshape(nx * value.shape[0], value.shape[1])


def direct_gather_z(value):
    nz = lax.axis_size("hz")
    z = lax.axis_index("hz")
    got = [value]
    for shift in range(1, nz):
        got.append(lax.ppermute(value, "hz", [(src, (src + shift) % nz) for src in range(nz)]))
    stacked = jnp.take(jnp.stack(got), (z - jnp.arange(nz)) % nz, axis=0)
    return stacked.reshape(nz * value.shape[0], value.shape[1])


def gather_over_head(value):
    return ring_gather_x(direct_gather_z(value))


def normalize_rows(layer_sum, mlp_gain):
    mean_square = jnp.mean(layer_sum * layer_sum, axis=1, keepdims=True)
    return (layer_sum * lax.rsqrt(mean_square + epsilon) * mlp_gain).astype(jnp.bfloat16)


def shards(
    x_in,
    z_in,
    bc,
    dt_raw,
    dt_bias,
    decay_rate,
    d_skip,
    norm_gain,
    out_weight,
    resid,
    mlp_gain,
    gate_weight,
    up_weight,
    down_weight,
):
    out_full, down_full = (
        lax.all_gather(out_weight, SEQ, axis=1, tiled=True),
        lax.all_gather(down_weight, SEQ, axis=1, tiled=True),
    )
    head_count = dt_raw.shape[0]
    length = dt_raw.shape[1]
    head_width = x_in.shape[1] // head_count
    step_size = jax.nn.softplus(dt_raw + dt_bias[:, None])
    log_decay = -decay_rate[:, None] * step_size
    x_heads = x_in.reshape(length, head_count, head_width)
    local_out, local_state = block_scan(x_heads, bc[0], bc[1], step_size, log_decay, BLOCK)
    running = jnp.cumsum(log_decay, axis=1)
    group_decay = jnp.exp(running[:, -1])
    entering = entering_state(group_decay, local_state)
    carried = jnp.einsum(
        "tn,hpn->thp", bc[1].astype(jnp.float32), entering, precision=lax.Precision.HIGHEST
    )
    carried = carried * jnp.exp(running).T[:, :, None]
    ssd_out = local_out + carried + d_skip[None, :, None] * x_heads.astype(jnp.float32)
    gated_out = ssd_out.reshape(length, head_count * head_width) * jax.nn.silu(
        z_in.astype(jnp.float32)
    )
    row_squares = jnp.sum(gated_out * gated_out, axis=1)
    gated_scaled = (gated_out * norm_gain).astype(jnp.bfloat16)
    head_n = lax.axis_size("hx") * lax.axis_size("hz")
    chunks = 1
    rows_per = length // head_n // chunks
    width = out_full.shape[1]
    gated_parts = gated_scaled.reshape(head_n, chunks, rows_per, -1)
    square_parts = row_squares.reshape(head_n, chunks, rows_per)
    resid_parts = resid.reshape(chunks, rows_per, -1)

    def packed_rows(chunk):
        chunk_rows = gated_parts[:, chunk].reshape(head_n * rows_per, -1)
        chunk_squares = square_parts[:, chunk].reshape(head_n * rows_per)
        partial_value = jnp.dot(chunk_rows, out_full, preferred_element_type=jnp.float32)
        sq_hi = chunk_squares.astype(jnp.bfloat16)
        sq_lo = (chunk_squares - sq_hi.astype(jnp.float32)).astype(jnp.bfloat16)
        extra = (
            jnp.zeros((head_n * rows_per, 128), jnp.bfloat16).at[:, 0].set(sq_hi).at[:, 1].set(sq_lo)
        )
        return jnp.concatenate([partial_value.astype(jnp.bfloat16), extra], axis=1)

    def finish_rows(reduced, chunk):
        part_rows = reduced[:, :width]
        part_squares = reduced[:, width] + reduced[:, width + 1]
        layer_sum = (
            resid_parts[chunk].astype(jnp.float32)
            + part_rows * lax.rsqrt(part_squares / INNER + epsilon)[:, None]
        )
        return layer_sum, normalize_rows(layer_sum, mlp_gain)

    def mlp_rows(rows_piece, down_full):
        gate_part = jnp.dot(rows_piece, gate_weight, preferred_element_type=jnp.float32)
        up_part = jnp.dot(rows_piece, up_weight, preferred_element_type=jnp.float32)
        hidden = (jax.nn.silu(gate_part) * up_part).astype(jnp.bfloat16)
        mlp_part = jnp.dot(hidden, down_full, preferred_element_type=jnp.float32)
        return sum_over_head(mlp_part.astype(jnp.bfloat16))

    packs = [packed_rows(chunk) for chunk in range(chunks)]
    normed_rows = []
    sums = []
    for chunk in range(chunks):
        pack = packs[chunk]
        if chunk > 0:
            pack, normed_rows[-1] = lax.optimization_barrier((pack, normed_rows[-1]))
        reduced = sum_over_head(pack)
        if chunk == 0:
            reduced, down_full = lax.optimization_barrier((reduced, down_full))
        layer_sum, normed = finish_rows(reduced, chunk)
        sums.append(layer_sum)
        normed_rows.append(normed)
    gathered = []
    for chunk in range(chunks):
        gathered.append(gather_over_head(normed_rows[chunk]))
        if chunk + 1 < chunks:
            gathered[-1], normed_rows[chunk + 1] = lax.optimization_barrier(
                (gathered[-1], normed_rows[chunk + 1])
            )
    outs = [sums[c] + mlp_rows(gathered[c], down_full) for c in range(chunks)]
    return jnp.concatenate(outs, axis=0).astype(jnp.bfloat16)


def solution(mesh):
    seq_n, head_n = mesh.devices.shape
    devices = mesh.devices.reshape(seq_n // 4, 2, 2, 4, head_n // 4)
    mesh = jax.sharding.Mesh(devices, ("sy", "sz", "sc", "hx", "hz"))
    head = ("hx", "hz")
    in_specs = (
        P(SEQ, head),
        P(SEQ, head),
        P(None, SEQ, None),
        P(head, SEQ),
        P(head),
        P(head),
        P(head),
        P(head),
        P(head, SEQ),
        P(SEQ + head, None),
        P(),
        P(None, head),
        P(None, head),
        P(head, SEQ),
    )
    out_specs = P(SEQ + head, None)
    return jax.shard_map(shards, mesh=mesh, in_specs=in_specs, out_specs=out_specs, check_vma=False)
```

```python
import jax
import jax.numpy as jnp
from jax import lax
from jax.sharding import PartitionSpec as P

BLOCK = 256
INNER = 8192


epsilon = 1e-05
SEQ = ("sy", "sz", "sc")


def block_scan(x_heads, b_rows, c_rows, step_size, log_decay, block_len):
    length, head_count, head_width = x_heads.shape
    state_size = b_rows.shape[1]
    block_count = length // block_len
    lower_mask = jnp.tril(jnp.ones((block_len, block_len), dtype=bool))
    carry_state = jnp.zeros((head_count, head_width, state_size), jnp.float32)
    outs = []
    for blk in range(block_count):
        rows = slice(blk * block_len, (blk + 1) * block_len)
        x_block = x_heads[rows]
        b_block = b_rows[rows]
        c_block = c_rows[rows]
        d_block = step_size[:, rows]
        a_block = log_decay[:, rows]
        cumulative = jnp.cumsum(a_block, axis=1)
        gap_values = jnp.where(
            lower_mask[None], cumulative[:, :, None] - cumulative[:, None, :], -jnp.inf
        )
        scores = jnp.dot(c_block, b_block.T, preferred_element_type=jnp.float32)
        mixing = (jnp.exp(gap_values) * scores[None] * d_block[:, None, :]).astype(jnp.bfloat16)
        within = jnp.einsum("hij,jhp->ihp", mixing, x_block, preferred_element_type=jnp.float32)
        if blk > 0:
            carried = jnp.einsum(
                "in,hpn->ihp", c_block.astype(jnp.float32), carry_state,
                precision=lax.Precision.HIGHEST,
            )
            within = within + carried * jnp.exp(cumulative).T[:, :, None]
        last_cum = cumulative[:, -1:]
        inject = (
            (jnp.exp(last_cum - cumulative) * d_block)[:, :, None]
            * b_block.astype(jnp.float32)[None]
        ).astype(jnp.bfloat16)
        added = jnp.einsum("jhp,hjn->hpn", x_block, inject, preferred_element_type=jnp.float32)
        carry_state = jnp.exp(last_cum)[:, :, None] * carry_state + added
        outs.append(within)
    return jnp.concatenate(outs, axis=0), carry_state


def combine(first, second):
    (d1, s1), (d2, s2) = first, second
    return d1 * d2, d2[:, None, None] * s1 + s2


def send(pair, pairs, axes):
    return tuple(lax.ppermute(v, axes, pairs) for v in pair)


def entering_state(group_decay, local_state):
    block = ("sz", "sc")
    j = lax.axis_index("sz") * 2 + lax.axis_index("sc")
    y = lax.axis_index("sy")
    ny = lax.axis_size("sy")
    own = (group_decay, local_state)
    ident = (jnp.ones_like(group_decay), jnp.zeros_like(local_state))

    def pick(cond, a, b):
        return tuple(jnp.where(cond, u, v) for u, v in zip(a, b))

    got = send(own, [(0, 1), (2, 3)], block)
    pair_agg = combine(got, own)
    lower = send(pair_agg, [(1, 2)], block)
    lower3 = send(lower, [(2, 3)], block)
    inner = pick(j == 1, got, ident)
    inner = pick(j == 2, lower, inner)
    inner = pick(j == 3, combine(lower3, got), inner)
    block_agg = combine(lower3, pair_agg)
    full = SEQ
    before = ident
    for k in range(ny - 1, 0, -1):
        pairs = [(4 * src + 3, 4 * (src + k) + 3) for src in range(ny - k)]
        got_k = send(block_agg, pairs, full)
        before = combine(before, pick(y >= k, got_k, ident))
    to_2 = send(before, [(3, 2)], block)
    to_1 = send(before, [(3, 1)], block)
    to_0 = send(to_1, [(1, 0)], block)
    prefix = pick(j == 3, before, to_0)
    prefix = pick(j == 2, to_2, prefix)
    prefix = pick(j == 1, to_1, prefix)
    return combine(prefix, inner)[1]


def ring_sum_x(pieces):
    nx = pieces.shape[0]
    x = lax.axis_index("hx")
    half = pieces.shape[2] // 2
    ways = ((1, pieces[:, :, :half]), (-1, pieces[:, :, half:]))
    accs = []
    for way, part in ways:
        pairs = [(src, (src + way) % nx) for src in range(nx)]
        acc = jnp.take(part, (x - way) % nx, axis=0).astype(jnp.float32)
        for step in range(nx - 1):
            got = lax.ppermute(acc.astype(jnp.bfloat16), "hx", pairs)
            chunk = (x - way * (step + 2)) % nx
            acc = got.astype(jnp.float32) + jnp.take(part, chunk, axis=0).astype(jnp.float32)
        accs.append(acc)
    return jnp.concatenate(accs, axis=1)


def sum_over_head(value):
    nx, nz = lax.axis_size("hx"), lax.axis_size("hz")
    pieces = value.reshape(nx, nz, value.shape[0] // (nx * nz), value.shape[1])
    pieces = ring_sum_x(pieces).astype(jnp.bfloat16)
    pieces = lax.all_to_all(pieces, "hz", 0, 0, tiled=False)
    return jnp.sum(pieces.astype(jnp.float32), axis=0)


def ring_gather_x(value):
    nx = lax.axis_size("hx")
    x = lax.axis_index("hx")
    half = value.shape[0] // 2
    slots = jnp.arange(nx)
    outs = []
    for way, part in ((1, value[:half]), (-1, value[half:])):
        pairs = [(src, (src + way) % nx) for src in range(nx)]
        got = [part]
        for step in range(nx - 1):
            got.append(lax.ppermute(got[-1], "hx", pairs))
        stacked = jnp.stack(got)
        outs.append(jnp.take(stacked, (way * (x - slots)) % nx, axis=0))
    return jnp.concatenate(outs, axis=1).reshape(nx * value.shape[0], value.shape[1])


def gather_z(value):
    nz = lax.axis_size("hz")
    copies = jnp.broadcast_to(value[None], (nz,) + value.shape)
    got = lax.all_to_all(copies, "hz", 0, 0, tiled=False)
    return got.reshape(nz * value.shape[0], value.shape[1])


def gather_over_head(value):
    return ring_gather_x(gather_z(value))


def normalize_rows(layer_sum, mlp_gain):
    mean_square = jnp.mean(layer_sum * layer_sum, axis=1, keepdims=True)
    return (layer_sum * lax.rsqrt(mean_square + epsilon) * mlp_gain).astype(jnp.bfloat16)


def shards(
    x_in,
    z_in,
    bc,
    dt_raw,
    dt_bias,
    decay_rate,
    d_skip,
    norm_gain,
    out_weight,
    resid,
    mlp_gain,
    gate_weight,
    up_weight,
    down_weight,
):
    out_full, down_full = (
        lax.all_gather(out_weight, SEQ, axis=1, tiled=True),
        lax.all_gather(down_weight, SEQ, axis=1, tiled=True),
    )
    head_count = dt_raw.shape[0]
    length = dt_raw.shape[1]
    head_width = x_in.shape[1] // head_count
    step_size = jax.nn.softplus(dt_raw + dt_bias[:, None])
    log_decay = -decay_rate[:, None] * step_size
    x_heads = x_in.reshape(length, head_count, head_width)
    local_out, local_state = block_scan(x_heads, bc[0], bc[1], step_size, log_decay, BLOCK)
    running = jnp.cumsum(log_decay, axis=1)
    group_decay = jnp.exp(running[:, -1])
    entering = entering_state(group_decay, local_state)
    carried = jnp.einsum(
        "tn,hpn->thp", bc[1].astype(jnp.float32), entering, precision=lax.Precision.HIGHEST
    )
    carried = carried * jnp.exp(running).T[:, :, None]
    ssd_out = local_out + carried + d_skip[None, :, None] * x_heads.astype(jnp.float32)
    gated_out = ssd_out.reshape(length, head_count * head_width) * jax.nn.silu(
        z_in.astype(jnp.float32)
    )
    row_squares = jnp.sum(gated_out * gated_out, axis=1)
    gated_scaled = (gated_out * norm_gain).astype(jnp.bfloat16)
    head_n = lax.axis_size("hx") * lax.axis_size("hz")
    chunks = 1
    rows_per = length // head_n // chunks
    width = out_full.shape[1]
    gated_parts = gated_scaled.reshape(head_n, chunks, rows_per, -1)
    square_parts = row_squares.reshape(head_n, chunks, rows_per)
    resid_parts = resid.reshape(chunks, rows_per, -1)

    def packed_rows(chunk):
        chunk_rows = gated_parts[:, chunk].reshape(head_n * rows_per, -1)
        chunk_squares = square_parts[:, chunk].reshape(head_n * rows_per)
        partial_value = jnp.dot(chunk_rows, out_full, preferred_element_type=jnp.float32)
        sq_hi = chunk_squares.astype(jnp.bfloat16)
        sq_lo = (chunk_squares - sq_hi.astype(jnp.float32)).astype(jnp.bfloat16)
        extra = (
            jnp.zeros((head_n * rows_per, 128), jnp.bfloat16).at[:, 0].set(sq_hi).at[:, 1].set(sq_lo)
        )
        return jnp.concatenate([partial_value.astype(jnp.bfloat16), extra], axis=1)

    def finish_rows(reduced, chunk):
        part_rows = reduced[:, :width]
        part_squares = reduced[:, width] + reduced[:, width + 1]
        layer_sum = (
            resid_parts[chunk].astype(jnp.float32)
            + part_rows * lax.rsqrt(part_squares / INNER + epsilon)[:, None]
        )
        return layer_sum, normalize_rows(layer_sum, mlp_gain)

    def mlp_rows(rows_piece, down_full):
        gate_part = jnp.dot(rows_piece, gate_weight, preferred_element_type=jnp.float32)
        up_part = jnp.dot(rows_piece, up_weight, preferred_element_type=jnp.float32)
        hidden = (jax.nn.silu(gate_part) * up_part).astype(jnp.bfloat16)
        mlp_part = jnp.dot(hidden, down_full, preferred_element_type=jnp.float32)
        return sum_over_head(mlp_part.astype(jnp.bfloat16))

    packs = [packed_rows(chunk) for chunk in range(chunks)]
    normed_rows = []
    sums = []
    for chunk in range(chunks):
        pack = packs[chunk]
        if chunk > 0:
            pack, normed_rows[-1] = lax.optimization_barrier((pack, normed_rows[-1]))
        reduced = sum_over_head(pack)
        if chunk == 0:
            reduced, down_full = lax.optimization_barrier((reduced, down_full))
        layer_sum, normed = finish_rows(reduced, chunk)
        sums.append(layer_sum)
        normed_rows.append(normed)
    gathered = []
    for chunk in range(chunks):
        gathered.append(gather_over_head(normed_rows[chunk]))
        if chunk + 1 < chunks:
            gathered[-1], normed_rows[chunk + 1] = lax.optimization_barrier(
                (gathered[-1], normed_rows[chunk + 1])
            )
    outs = [sums[c] + mlp_rows(gathered[c], down_full) for c in range(chunks)]
    return jnp.concatenate(outs, axis=0).astype(jnp.bfloat16)


def solution(mesh):
    seq_n, head_n = mesh.devices.shape
    devices = mesh.devices.reshape(seq_n // 4, 2, 2, 4, head_n // 4)
    mesh = jax.sharding.Mesh(devices, ("sy", "sz", "sc", "hx", "hz"))
    head = ("hx", "hz")
    in_specs = (
        P(SEQ, head),
        P(SEQ, head),
        P(None, SEQ, None),
        P(head, SEQ),
        P(head),
        P(head),
        P(head),
        P(head),
        P(head, SEQ),
        P(SEQ + head, None),
        P(),
        P(None, head),
        P(None, head),
        P(head, SEQ),
    )
    out_specs = P(SEQ + head, None)
    return jax.shard_map(shards, mesh=mesh, in_specs=in_specs, out_specs=out_specs, check_vma=False)
```
